32 devices in a mesh: rec: 2 (over core), space: 16 (over z, y, x).
Axes of the slice: x: 2, y: 2, z: 4, core: 2. Of those that a mesh axis runs over, the one named last changes fastest.
Arguments:
- footprints: bfloat16 [32, 120, 8400], P(('rec', 'space')), may hold values from 0 to 1
- time_cov: bfloat16 [120, 120], replicated, may hold values from -1 to 3
- lat_cov: bfloat16 [70, 70], replicated, may hold values from -1 to 3
- lon_cov: bfloat16 [120, 120], replicated, may hold values from -1 to 3
Outputs:
- gram: float32 [32, 32], P(('rec', 'space'))
The draws below stay inside these ranges and needn't reach their ends.
All inputs are finite; a program needn't handle non-finite values.
Results may differ from the reference program's by a relative error of at most 0.0003.
Values may be sent and summed in bfloat16 or wider, within the bound.
No kernel may reach another device: no remote copies, remote signals or barrier semaphores. Data moves between devices by JAX's collectives and lax.ppermute only.
A program may use at most 64 MiB of HBM per device.

```python
import math
import jax
import jax.numpy as jnp
from jax import lax

T_SIZE = 120
LAT = 70
LON = 120
CELLS = 8400
R = 32


def covariance_from(off_raw, diag_key, size):
    off_sym = 0.75 * (off_raw + off_raw.T) / size
    diagonal = jax.random.uniform(diag_key, (size,), jnp.float32, 1.5, 3.0)
    on_diag = jnp.arange(size)[:, None] == jnp.arange(size)[None, :]
    return jnp.where(on_diag, jnp.broadcast_to(diagonal[None, :], (size, size)), off_sym)


def draw_factor(key, size, salt):
    key_off = jax.random.fold_in(key, salt)
    key_diag = jax.random.fold_in(key, salt + 1)
    off_raw = jax.random.uniform(key_off, (size, size), jnp.float32, -1.0, 1.0)
    return covariance_from(off_raw, key_diag, size)


def draw_time_cov(key, part):
    return draw_factor(key, T_SIZE, 11).astype(jnp.bfloat16)


def draw_lat_cov(key, part):
    return draw_factor(key, LAT, 23).astype(jnp.bfloat16)


def draw_lon_cov(key, part):
    return draw_factor(key, LON, 37).astype(jnp.bfloat16)


def draw_footprints(key, part):
    key_time = jax.random.fold_in(key, 101)
    key_lat = jax.random.fold_in(key, 103)
    key_lon = jax.random.fold_in(key, 105)
    key_jitter_lat = jax.random.fold_in(key, 107)
    key_jitter_lon = jax.random.fold_in(key, 109)
    key_decay = jax.random.fold_in(key, 111)
    key_width_lat = jax.random.fold_in(key, 113)
    key_width_lon = jax.random.fold_in(key, 115)
    key_amplitude = jax.random.fold_in(key, 117)
    key_rough = jax.random.fold_in(key, 119)
    site_count = (R + 3) // 4
    receptor = jnp.arange(R)
    cluster = receptor // 4
    base_time = jax.random.randint(key_time, (site_count,), T_SIZE // 2, T_SIZE - 3)
    time_of = base_time[cluster] + receptor % 4
    lat_site = jax.random.uniform(key_lat, (site_count,), jnp.float32, 0.0, LAT - 1.0)
    lon_site = jax.random.uniform(key_lon, (site_count,), jnp.float32, 0.0, LON - 1.0)
    lat_of = lat_site[cluster] + jax.random.uniform(key_jitter_lat, (R,), jnp.float32, -1.0, 1.0) * (LAT / 20.0)
    lon_of = lon_site[cluster] + jax.random.uniform(key_jitter_lon, (R,), jnp.float32, -1.0, 1.0) * (LON / 20.0)
    decay = jax.random.uniform(key_decay, (R,), jnp.float32, T_SIZE / 20.0, T_SIZE / 8.0)
    width_lat = jax.random.uniform(key_width_lat, (R,), jnp.float32, LAT / 14.0, LAT / 6.0)
    width_lon = jax.random.uniform(key_width_lon, (R,), jnp.float32, LON / 14.0, LON / 6.0)
    amplitude = jnp.exp(jax.random.uniform(key_amplitude, (R,), jnp.float32, math.log(0.5), math.log(1.5)))
    lag = (time_of[:, None] - jnp.arange(T_SIZE)[None, :]).astype(jnp.float32)
    weight_time = jnp.where(lag >= 0.0, jnp.exp(-jnp.maximum(lag, 0.0) / decay[:, None]), 0.0)
    lat_index = (jnp.arange(CELLS) // LON).astype(jnp.float32)
    lon_index = (jnp.arange(CELLS) % LON).astype(jnp.float32)
    lat_part = (lat_index[None, :] - lat_of[:, None]) / width_lat[:, None]
    lon_part = (lon_index[None, :] - lon_of[:, None]) / width_lon[:, None]
    plume = 1.0 / (1.0 + lat_part * lat_part + lon_part * lon_part)
    time_total = 1.0 / (1.0 - jnp.exp(-2.0 / decay))
    space_total = math.pi * width_lat * width_lon + 1.0
    scale = jnp.sqrt(0.15 * amplitude / (time_total * space_total))
    rough = jnp.exp(jax.random.uniform(key_rough, (R, T_SIZE, CELLS), jnp.float32, math.log(0.2), math.log(2.0)))
    values = scale[:, None, None] * weight_time[:, :, None] * plume[:, None, :] * rough
    return jnp.minimum(values, 1.0).astype(jnp.bfloat16)


def setup_inputs(seed: int = 0) -> dict:
    splits = jax.random.split(jax.random.key(seed), 5)
    return {
        "footprints": draw_footprints(jax.random.fold_in(splits[4], 71), 0),
        "time_cov": draw_time_cov(jax.random.fold_in(splits[4], 71), 0),
        "lat_cov": draw_lat_cov(jax.random.fold_in(splits[4], 71), 0),
        "lon_cov": draw_lon_cov(jax.random.fold_in(splits[4], 71), 0),
    }


def weigh_footprint(footprint, time_cov, lat_cov, lon_cov):
    along_lon = jnp.dot(footprint.reshape(T_SIZE * LAT, LON), lon_cov, preferred_element_type=jnp.float32).astype(jnp.bfloat16)
    along_lat = jnp.einsum("tab,ac->tcb", along_lon.reshape(T_SIZE, LAT, LON).astype(jnp.float32), lat_cov.astype(jnp.float32)).astype(jnp.bfloat16)
    return jnp.dot(time_cov.T, along_lat.reshape(T_SIZE, CELLS), preferred_element_type=jnp.float32).astype(jnp.bfloat16)


def reference(footprints, time_cov, lat_cov, lon_cov):
    weighted = lax.map(lambda footprint: weigh_footprint(footprint, time_cov, lat_cov, lon_cov), footprints)

    def accumulate(time_index, running):
        weighted_slice = lax.dynamic_index_in_dim(weighted, time_index, 1, keepdims=False)
        plain_slice = lax.dynamic_index_in_dim(footprints, time_index, 1, keepdims=False)
        return running + jnp.dot(weighted_slice, plain_slice.T, preferred_element_type=jnp.float32)

    return lax.fori_loop(0, T_SIZE, accumulate, jnp.zeros((R, R), jnp.float32))
```

```python
import jax
import jax.numpy as jnp
from jax import lax
from jax.sharding import PartitionSpec as P

ROW_TILE = 16
LANE = 128


def weigh_footprints(footprints, time_cov, lat_cov, lon_cov):
    receptors_here, time_count, cell_count = footprints.shape
    lat_count = lat_cov.shape[0]
    lon_count = lon_cov.shape[0]
    along_lon = jnp.dot(
        footprints.reshape(receptors_here * time_count * lat_count, lon_count),
        lon_cov,
        preferred_element_type=jnp.float32,
    ).astype(jnp.bfloat16)
    along_lat = jnp.einsum(
        "rab,ac->rcb",
        along_lon.reshape(receptors_here * time_count, lat_count, lon_count),
        lat_cov,
        preferred_element_type=jnp.float32,
    ).astype(jnp.bfloat16)
    return jnp.einsum(
        "rtc,ts->rsc",
        along_lat.reshape(receptors_here, time_count, cell_count),
        time_cov,
        preferred_element_type=jnp.float32,
    ).astype(jnp.bfloat16)


def chunk_geometry(time_count, cell_count, chunks):
    row_tiles = -(-time_count // ROW_TILE)
    col_tiles = -(-cell_count // LANE)
    if chunks % row_tiles == 0:
        per_row = chunks // row_tiles
        col_tiles = -(-col_tiles // per_row) * per_row
    else:
        assert row_tiles % chunks == 0
        per_row = 1
    return row_tiles, col_tiles, per_row


def to_chunks(values, chunks):
    time_count, cell_count = values.shape
    row_tiles, col_tiles, per_row = chunk_geometry(time_count, cell_count, chunks)
    rows = row_tiles * ROW_TILE
    cols = col_tiles * LANE
    padded = jnp.pad(values, ((0, rows - time_count), (0, cols - cell_count)))
    if per_row > 1:
        blocks = padded.reshape(row_tiles, ROW_TILE, per_row, cols // per_row)
        return blocks.transpose(0, 2, 1, 3).reshape(chunks, ROW_TILE, cols // per_row)
    return padded.reshape(chunks, rows // chunks, cols)


def local(footprints, time_cov, lat_cov, lon_cov):
    space_count = lax.axis_size("space")
    rec_index = lax.axis_index("rec")
    plain = to_chunks(footprints[0], space_count)
    plain_here = lax.all_to_all(plain, "space", split_axis=0, concat_axis=0, tiled=True)
    weighted = to_chunks(weigh_footprints(footprints, time_cov, lat_cov, lon_cov)[0], space_count)
    weighted_here = lax.all_to_all(weighted, "space", split_axis=0, concat_axis=0, tiled=True)
    rec_count = lax.axis_size("rec")
    contract = (((1, 2), (1, 2)), ((), ()))
    if rec_count == 1:
        partial_value = lax.dot_general(weighted_here, plain_here, contract, preferred_element_type=jnp.float32)
    else:
        gathered = lax.all_gather(plain_here, "rec", axis=0, tiled=True)
        partial_value = lax.dot_general(weighted_here, gathered, contract, preferred_element_type=jnp.float32)
    return lax.psum_scatter(partial_value, "space", scatter_dimension=0, tiled=True)


def solution(mesh):
    in_specs = (P(("rec", "space"), None, None), P(), P(), P())
    out_specs = P(("rec", "space"), None)
    return jax.shard_map(local, mesh=mesh, in_specs=in_specs, out_specs=out_specs, check_vma=False)
```

```python
import jax
import jax.numpy as jnp
from jax import lax
from jax.sharding import PartitionSpec as P

ROW_TILE = 16
LANE = 128


def chunk_geometry(time_count, cell_count, chunks):
    row_tiles = -(-time_count // ROW_TILE)
    col_tiles = -(-cell_count // LANE)
    assert chunks % row_tiles == 0
    per_row = chunks // row_tiles
    col_tiles = -(-col_tiles // per_row) * per_row
    return row_tiles, col_tiles * LANE, per_row


def plain_chunks(values, chunks):
    time_count, cell_count = values.shape
    row_tiles, cols, per_row = chunk_geometry(time_count, cell_count, chunks)
    padded = jnp.pad(values, ((0, row_tiles * ROW_TILE - time_count), (0, cols - cell_count)))
    width = cols // per_row
    blocks = padded.reshape(row_tiles, ROW_TILE, per_row, width)
    return blocks.transpose(0, 2, 1, 3).reshape(chunks, ROW_TILE, width)


def weighted_chunks(footprint, time_cov, lat_cov, lon_cov, chunks):
    time_count, cell_count = footprint.shape
    lat_count = lat_cov.shape[0]
    lon_count = lon_cov.shape[0]
    row_tiles, cols, per_row = chunk_geometry(time_count, cell_count, chunks)
    along_lon = jnp.dot(
        footprint.reshape(time_count * lat_count, lon_count),
        lon_cov,
        preferred_element_type=jnp.float32,
    ).astype(jnp.bfloat16)
    along_lat = jnp.einsum(
        "tab,ac->tcb",
        along_lon.reshape(time_count, lat_count, lon_count),
        lat_cov,
        preferred_element_type=jnp.float32,
    ).astype(jnp.bfloat16)
    along_lat = jnp.pad(along_lat.reshape(time_count, cell_count), ((0, 0), (0, cols - cell_count)))
    width = cols // per_row
    time_padded = jnp.pad(time_cov, ((0, 0), (0, row_tiles * ROW_TILE - time_count)))
    weighted = jnp.einsum(
        "trq,thc->rhqc",
        time_padded.reshape(time_count, row_tiles, ROW_TILE),
        along_lat.reshape(time_count, per_row, width),
        preferred_element_type=jnp.float32,
    ).astype(jnp.bfloat16)
    return weighted.reshape(chunks, ROW_TILE, width)


def local(footprints, time_cov, lat_cov, lon_cov):
    space_count = lax.axis_size("space")
    rec_count = lax.axis_size("rec")
    rec_index = lax.axis_index("rec")
    plain = plain_chunks(footprints[0], space_count)
    plain_here = lax.all_to_all(plain, "space", split_axis=0, concat_axis=0, tiled=True)
    weighted = weighted_chunks(footprints[0], time_cov, lat_cov, lon_cov, space_count)
    weighted_here = lax.all_to_all(weighted, "space", split_axis=0, concat_axis=0, tiled=True)
    contract = (((1, 2), (1, 2)), ((), ()))
    group = plain_here.shape[0]
    partial_value = jnp.zeros((group, group * rec_count), jnp.float32)
    for shift in range(rec_count):
        if shift == 0:
            other = plain_here
        else:
            perm = [(i, (i + shift) % rec_count) for i in range(rec_count)]
            other = lax.ppermute(plain_here, "rec", perm)
        block = lax.dot_general(weighted_here, other, contract, preferred_element_type=jnp.float32)
        source = (rec_index + rec_count - shift) % rec_count
        partial_value = lax.dynamic_update_slice(partial_value, block, (0, source * group))
    spread = lax.all_to_all(partial_value, "space", split_axis=0, concat_axis=0, tiled=True)
    return jnp.sum(spread, axis=0, keepdims=True)


def solution(mesh):
    in_specs = (P(("rec", "space"), None, None), P(), P(), P())
    out_specs = P(("rec", "space"), None)
    return jax.shard_map(local, mesh=mesh, in_specs=in_specs, out_specs=out_specs, check_vma=False)
```

```python
import jax
import jax.numpy as jnp
from jax import lax
from jax.sharding import PartitionSpec as P

ROW_TILE = 16
LANE = 128


def chunk_geometry(time_count, cell_count, chunks):
    row_tiles = -(-time_count // ROW_TILE)
    col_tiles = -(-cell_count // LANE)
    assert chunks % row_tiles == 0
    per_row = chunks // row_tiles
    col_tiles = -(-col_tiles // per_row) * per_row
    return row_tiles, col_tiles * LANE, per_row


def plain_chunks(values, chunks):
    time_count, cell_count = values.shape
    row_tiles, cols, per_row = chunk_geometry(time_count, cell_count, chunks)
    padded = jnp.pad(values, ((0, row_tiles * ROW_TILE - time_count), (0, cols - cell_count)))
    width = cols // per_row
    pieces = [
        padded[row * ROW_TILE:(row + 1) * ROW_TILE, part * width:(part + 1) * width]
        for row in range(row_tiles)
        for part in range(per_row)
    ]
    return jnp.concatenate(pieces, axis=0).reshape(chunks, ROW_TILE, width)


def weighted_chunks(footprint, time_cov, lat_cov, lon_cov, chunks):
    time_count, cell_count = footprint.shape
    lat_count = lat_cov.shape[0]
    lon_count = lon_cov.shape[0]
    row_tiles, cols, per_row = chunk_geometry(time_count, cell_count, chunks)
    along_lon = jnp.dot(
        footprint.reshape(time_count * lat_count, lon_count),
        lon_cov,
        preferred_element_type=jnp.float32,
    ).astype(jnp.bfloat16)
    along_lat = jnp.einsum(
        "tab,ac->tcb",
        along_lon.reshape(time_count, lat_count, lon_count),
        lat_cov,
        preferred_element_type=jnp.float32,
    ).astype(jnp.bfloat16)
    along_lat = jnp.pad(along_lat.reshape(time_count, cell_count), ((0, 0), (0, cols - cell_count)))
    width = cols // per_row
    time_padded = jnp.pad(time_cov, ((0, 0), (0, row_tiles * ROW_TILE - time_count)))
    weighted = jnp.einsum(
        "trq,thc->rhqc",
        time_padded.reshape(time_count, row_tiles, ROW_TILE),
        along_lat.reshape(time_count, per_row, width),
        preferred_element_type=jnp.float32,
    ).astype(jnp.bfloat16)
    return weighted.reshape(chunks, ROW_TILE, width)


def local(footprints, time_cov, lat_cov, lon_cov):
    space_count = lax.axis_size("space")
    rec_count = lax.axis_size("rec")
    rec_index = lax.axis_index("rec")
    plain = plain_chunks(footprints[0], space_count)
    plain_here = lax.all_to_all(plain, "space", split_axis=0, concat_axis=0, tiled=True)
    weighted = weighted_chunks(footprints[0], time_cov, lat_cov, lon_cov, space_count)
    weighted_here = lax.all_to_all(weighted, "space", split_axis=0, concat_axis=0, tiled=True)
    contract = (((1, 2), (1, 2)), ((), ()))
    group = plain_here.shape[0]
    received = [plain_here]
    for shift in range(1, rec_count):
        perm = [(i, (i + shift) % rec_count) for i in range(rec_count)]
        received.append(lax.ppermute(plain_here, "rec", perm))
    ordered = []
    for g in range(rec_count):
        choice = received[0]
        for shift in range(1, rec_count):
            choice = jnp.where((rec_index + rec_count - shift) % rec_count == g, received[shift], choice)
        ordered.append(choice)
    everyone = jnp.concatenate(ordered, axis=0)
    partial_value = lax.dot_general(weighted_here, everyone, contract, preferred_element_type=jnp.float32)
    spread = lax.all_to_all(partial_value, "space", split_axis=0, concat_axis=0, tiled=True)
    return jnp.sum(spread, axis=0, keepdims=True)


def solution(mesh):
    in_specs = (P(("rec", "space"), None, None), P(), P(), P())
    out_specs = P(("rec", "space"), None)
    return jax.shard_map(local, mesh=mesh, in_specs=in_specs, out_specs=out_specs, check_vma=False)
```

```python
import jax
import jax.numpy as jnp
from jax import lax
from jax.sharding import PartitionSpec as P

ROW_TILE = 16
LANE = 128


def dense_chunks(values, chunks):
    time_count, cell_count = values.shape
    col_tiles = cell_count // LANE
    per = col_tiles // chunks
    main_cols = per * chunks * LANE
    main = values[:, :main_cols].reshape(time_count, chunks, per, LANE)
    main = main.transpose(1, 2, 0, 3).reshape(chunks, per * time_count, LANE)
    rest_tiles = -(-(cell_count - main_cols) // LANE)
    rest_rows = rest_tiles * time_count
    share = -(-rest_rows // chunks)
    rest = jnp.pad(values[:, main_cols:], ((0, 0), (0, rest_tiles * LANE - (cell_count - main_cols))))
    rest = rest.reshape(time_count, rest_tiles, LANE).transpose(1, 0, 2).reshape(rest_rows, LANE)
    rest = jnp.pad(rest, ((0, share * chunks - rest_rows), (0, 0))).reshape(chunks, share, LANE)
    rows = per * time_count + share
    padded_rows = -(-rows // ROW_TILE) * ROW_TILE
    pieces = [main, rest]
    if padded_rows > rows:
        pieces.append(jnp.zeros((chunks, padded_rows - rows, LANE), values.dtype))
    return jnp.concatenate(pieces, axis=1)


def weighted_full(footprint, time_cov, lat_cov, lon_cov):
    time_count, cell_count = footprint.shape
    lat_count = lat_cov.shape[0]
    lon_count = lon_cov.shape[0]
    along_lon = jnp.dot(
        footprint.reshape(time_count * lat_count, lon_count),
        lon_cov,
        preferred_element_type=jnp.float32,
    ).astype(jnp.bfloat16)
    along_lat = jnp.einsum(
        "tab,ac->tcb",
        along_lon.reshape(time_count, lat_count, lon_count),
        lat_cov,
        preferred_element_type=jnp.float32,
    ).astype(jnp.bfloat16)
    return jnp.dot(
        time_cov.T, along_lat.reshape(time_count, cell_count), preferred_element_type=jnp.float32
    ).astype(jnp.bfloat16)


def local(footprints, time_cov, lat_cov, lon_cov):
    space_count = lax.axis_size("space")
    rec_count = lax.axis_size("rec")
    rec_index = lax.axis_index("rec")
    plain = dense_chunks(footprints[0], space_count)
    plain, footprint = lax.optimization_barrier((plain, footprints[0]))
    plain_here = lax.all_to_all(plain, "space", split_axis=0, concat_axis=0, tiled=True)
    weighted = dense_chunks(weighted_full(footprint, time_cov, lat_cov, lon_cov), space_count)
    weighted_here = lax.all_to_all(weighted, "space", split_axis=0, concat_axis=0, tiled=True)
    contract = (((1, 2), (1, 2)), ((), ()))
    group = plain_here.shape[0]
    received = [plain_here]
    for shift in range(1, rec_count):
        perm = [(i, (i + shift) % rec_count) for i in range(rec_count)]
        received.append(lax.ppermute(plain_here, "rec", perm))
    ordered = []
    for g in range(rec_count):
        choice = received[0]
        for shift in range(1, rec_count):
            choice = jnp.where((rec_index + rec_count - shift) % rec_count == g, received[shift], choice)
        ordered.append(choice)
    everyone = jnp.concatenate(ordered, axis=0)
    partial_value = lax.dot_general(weighted_here, everyone, contract, preferred_element_type=jnp.float32)
    spread = lax.all_to_all(partial_value, "space", split_axis=0, concat_axis=0, tiled=True)
    return jnp.sum(spread, axis=0, keepdims=True)


def solution(mesh):
    in_specs = (P(("rec", "space"), None, None), P(), P(), P())
    out_specs = P(("rec", "space"), None)
    return jax.shard_map(local, mesh=mesh, in_specs=in_specs, out_specs=out_specs, check_vma=False)
```

```python
import jax
import jax.numpy as jnp
from jax import lax
from jax.sharding import PartitionSpec as P

ROW_TILE = 16
LANE = 128


def layout_of(time_count, cell_count, chunks):
    col_tiles = cell_count // LANE
    per = col_tiles // chunks
    main_cols = per * chunks * LANE
    full_rows = (time_count // ROW_TILE) * ROW_TILE
    rest_rows = (time_count - full_rows) * (main_cols // LANE)
    rest_rows += time_count * (-(-(cell_count - main_cols) // LANE))
    share = -(-rest_rows // chunks)
    rows = per * full_rows + share
    padded_rows = -(-rows // ROW_TILE) * ROW_TILE
    return per, main_cols, full_rows, share, padded_rows - rows


def rest_chunks(low, right, chunks, share):
    parts = []
    if low.shape[0]:
        height = low.shape[0]
        parts.append(low.reshape(height, -1, LANE).transpose(1, 0, 2).reshape(-1, LANE))
    if right.shape[1]:
        height, width = right.shape
        tiles = -(-width // LANE)
        right = jnp.pad(right, ((0, 0), (0, tiles * LANE - width)))
        parts.append(right.reshape(height, tiles, LANE).transpose(1, 0, 2).reshape(-1, LANE))
    rest = jnp.concatenate(parts, axis=0)
    rest = jnp.pad(rest, ((0, share * chunks - rest.shape[0]), (0, 0)))
    return rest.reshape(chunks, share, LANE)


def assemble(main, rest, extra, chunks, dtype):
    pieces = [main, rest]
    if extra:
        pieces.append(jnp.zeros((chunks, extra, LANE), dtype))
    return jnp.concatenate(pieces, axis=1)


def dense_chunks(values, chunks):
    time_count, cell_count = values.shape
    per, main_cols, full_rows, share, extra = layout_of(time_count, cell_count, chunks)
    main = jnp.stack([values[:full_rows, j * LANE:(j + 1) * LANE] for j in range(chunks * per)])
    main = main.reshape(chunks, per * full_rows, LANE)
    rest = rest_chunks(values[full_rows:, :main_cols], values[:, main_cols:], chunks, share)
    return assemble(main, rest, extra, chunks, values.dtype)


def weighted_dense_chunks(footprint, time_cov, lat_cov, lon_cov, chunks):
    time_count, cell_count = footprint.shape
    lat_count = lat_cov.shape[0]
    lon_count = lon_cov.shape[0]
    per, main_cols, full_rows, share, extra = layout_of(time_count, cell_count, chunks)
    along_lon = jnp.dot(
        footprint.reshape(time_count * lat_count, lon_count),
        lon_cov,
        preferred_element_type=jnp.float32,
    ).astype(jnp.bfloat16)
    along_lat = jnp.einsum(
        "tab,ac->tcb",
        along_lon.reshape(time_count, lat_count, lon_count),
        lat_cov,
        preferred_element_type=jnp.float32,
    ).astype(jnp.bfloat16)
    along_lat = along_lat.reshape(time_count, cell_count)
    main = along_lat[:, :main_cols].reshape(time_count, chunks * per, LANE)
    main = jnp.einsum("ts,tjl->jsl", time_cov[:, :full_rows], main, preferred_element_type=jnp.float32)
    main = main.astype(jnp.bfloat16).reshape(chunks, per * full_rows, LANE)
    low = jnp.dot(time_cov[:, full_rows:].T, along_lat[:, :main_cols], preferred_element_type=jnp.float32)
    right = jnp.dot(time_cov.T, along_lat[:, main_cols:], preferred_element_type=jnp.float32)
    rest = rest_chunks(low.astype(jnp.bfloat16), right.astype(jnp.bfloat16), chunks, share)
    return assemble(main, rest, extra, chunks, jnp.bfloat16)


def local(footprints, time_cov, lat_cov, lon_cov):
    space_count = lax.axis_size("space")
    rec_count = lax.axis_size("rec")
    rec_index = lax.axis_index("rec")
    plain = dense_chunks(footprints[0], space_count)
    plain, footprint = lax.optimization_barrier((plain, footprints[0]))
    plain_here = lax.all_to_all(plain, "space", split_axis=0, concat_axis=0, tiled=True)
    weighted = weighted_dense_chunks(footprint, time_cov, lat_cov, lon_cov, space_count)
    weighted_here = lax.all_to_all(weighted, "space", split_axis=0, concat_axis=0, tiled=True)
    contract = (((1, 2), (1, 2)), ((), ()))
    group = plain_here.shape[0]
    received = [plain_here]
    for shift in range(1, rec_count):
        perm = [(i, (i + shift) % rec_count) for i in range(rec_count)]
        received.append(lax.ppermute(plain_here, "rec", perm))
    ordered = []
    for g in range(rec_count):
        choice = received[0]
        for shift in range(1, rec_count):
            choice = jnp.where((rec_index + rec_count - shift) % rec_count == g, received[shift], choice)
        ordered.append(choice)
    everyone = jnp.concatenate(ordered, axis=0)
    partial_value = lax.dot_general(weighted_here, everyone, contract, preferred_element_type=jnp.float32)
    spread = lax.all_to_all(partial_value, "space", split_axis=0, concat_axis=0, tiled=True)
    return jnp.sum(spread, axis=0, keepdims=True)


def solution(mesh):
    in_specs = (P(("rec", "space"), None, None), P(), P(), P())
    out_specs = P(("rec", "space"), None)
    return jax.shard_map(local, mesh=mesh, in_specs=in_specs, out_specs=out_specs, check_vma=False)
```

```python
import functools
import jax
import jax.numpy as jnp
from jax import lax
from jax.sharding import PartitionSpec as P
from jax.experimental import pallas as pl
from jax.experimental.pallas import tpu as pltpu

ROW_TILE = 16
LANE = 128


def layout_of(time_count, cell_count, chunks):
    col_tiles = cell_count // LANE
    per = col_tiles // chunks
    main_cols = per * chunks * LANE
    full_rows = (time_count // ROW_TILE) * ROW_TILE
    rest_rows = (time_count - full_rows) * (main_cols // LANE)
    rest_rows += time_count * (-(-(cell_count - main_cols) // LANE))
    share = -(-rest_rows // chunks)
    rows = per * full_rows + share
    padded_rows = -(-rows // ROW_TILE) * ROW_TILE
    return per, main_cols, full_rows, share, padded_rows - rows


def rest_chunks(low, right, chunks, share):
    parts = []
    if low.shape[0]:
        height = low.shape[0]
        parts.append(low.reshape(height, -1, LANE).transpose(1, 0, 2).reshape(-1, LANE))
    if right.shape[1]:
        height, width = right.shape
        tiles = -(-width // LANE)
        right = jnp.pad(right, ((0, 0), (0, tiles * LANE - width)))
        parts.append(right.reshape(height, tiles, LANE).transpose(1, 0, 2).reshape(-1, LANE))
    rest = jnp.concatenate(parts, axis=0)
    rest = jnp.pad(rest, ((0, share * chunks - rest.shape[0]), (0, 0)))
    return rest.reshape(chunks, share, LANE)


def assemble(main, rest, extra, chunks, dtype):
    pieces = [main, rest]
    if extra:
        pieces.append(jnp.zeros((chunks, extra, LANE), dtype))
    return jnp.concatenate(pieces, axis=1)


def pack_kernel(full_rows, per, values_ref, rest_ref, out_ref):
    chunks = out_ref.shape[0]
    for k in range(chunks):
        for q in range(per):
            j = k * per + q
            out_ref[k, q * full_rows:(q + 1) * full_rows, :] = values_ref[0:full_rows, j * LANE:(j + 1) * LANE]
        out_ref[k, per * full_rows:, :] = rest_ref[k]


def dense_chunks(values, chunks):
    time_count, cell_count = values.shape
    per, main_cols, full_rows, share, extra = layout_of(time_count, cell_count, chunks)
    rest = rest_chunks(values[full_rows:, :main_cols], values[:, main_cols:], chunks, share)
    if extra:
        rest = jnp.pad(rest, ((0, 0), (0, extra), (0, 0)))
    rows = per * full_rows + share + extra
    return pl.pallas_call(
        functools.partial(pack_kernel, full_rows, per),
        out_shape=jax.ShapeDtypeStruct((chunks, rows, LANE), values.dtype),
        in_specs=[pl.BlockSpec(memory_space=pltpu.VMEM)] * 2,
        out_specs=pl.BlockSpec(memory_space=pltpu.VMEM),
        cost_estimate=pl.CostEstimate(flops=0, transcendentals=0, bytes_accessed=4 * chunks * rows * LANE),
    )(values, rest)


def weighted_dense_chunks(footprint, time_cov, lat_cov, lon_cov, chunks):
    time_count, cell_count = footprint.shape
    lat_count = lat_cov.shape[0]
    lon_count = lon_cov.shape[0]
    per, main_cols, full_rows, share, extra = layout_of(time_count, cell_count, chunks)
    along_lon = jnp.dot(
        footprint.reshape(time_count * lat_count, lon_count),
        lon_cov,
        preferred_element_type=jnp.float32,
    ).astype(jnp.bfloat16)
    along_lat = jnp.einsum(
        "tab,ac->tcb",
        along_lon.reshape(time_count, lat_count, lon_count),
        lat_cov,
        preferred_element_type=jnp.float32,
    ).astype(jnp.bfloat16)
    along_lat = along_lat.reshape(time_count, cell_count)
    main = along_lat[:, :main_cols].reshape(time_count, chunks * per, LANE)
    main = jnp.einsum("ts,tjl->jsl", time_cov[:, :full_rows], main, preferred_element_type=jnp.float32)
    main = main.astype(jnp.bfloat16).reshape(chunks, per * full_rows, LANE)
    low = jnp.dot(time_cov[:, full_rows:].T, along_lat[:, :main_cols], preferred_element_type=jnp.float32)
    right = jnp.dot(time_cov.T, along_lat[:, main_cols:], preferred_element_type=jnp.float32)
    rest = rest_chunks(low.astype(jnp.bfloat16), right.astype(jnp.bfloat16), chunks, share)
    return assemble(main, rest, extra, chunks, jnp.bfloat16)


def local(footprints, time_cov, lat_cov, lon_cov):
    space_count = lax.axis_size("space")
    rec_count = lax.axis_size("rec")
    rec_index = lax.axis_index("rec")
    plain = dense_chunks(footprints[0], space_count)
    plain, footprint = lax.optimization_barrier((plain, footprints[0]))
    plain_here = lax.all_to_all(plain, "space", split_axis=0, concat_axis=0, tiled=True)
    weighted = weighted_dense_chunks(footprint, time_cov, lat_cov, lon_cov, space_count)
    weighted_here = lax.all_to_all(weighted, "space", split_axis=0, concat_axis=0, tiled=True)
    contract = (((1, 2), (1, 2)), ((), ()))
    group = plain_here.shape[0]
    received = [plain_here]
    for shift in range(1, rec_count):
        perm = [(i, (i + shift) % rec_count) for i in range(rec_count)]
        received.append(lax.ppermute(plain_here, "rec", perm))
    ordered = []
    for g in range(rec_count):
        choice = received[0]
        for shift in range(1, rec_count):
            choice = jnp.where((rec_index + rec_count - shift) % rec_count == g, received[shift], choice)
        ordered.append(choice)
    everyone = jnp.concatenate(ordered, axis=0)
    partial_value = lax.dot_general(weighted_here, everyone, contract, preferred_element_type=jnp.float32)
    spread = lax.all_to_all(partial_value, "space", split_axis=0, concat_axis=0, tiled=True)
    return jnp.sum(spread, axis=0, keepdims=True)


def solution(mesh):
    in_specs = (P(("rec", "space"), None, None), P(), P(), P())
    out_specs = P(("rec", "space"), None)
    return jax.shard_map(local, mesh=mesh, in_specs=in_specs, out_specs=out_specs, check_vma=False)
```

```python
import functools
import jax
import jax.numpy as jnp
from jax import lax
from jax.sharding import PartitionSpec as P
from jax.experimental import pallas as pl
from jax.experimental.pallas import tpu as pltpu

ROW_TILE = 16
LANE = 128


def layout_of(time_count, cell_count, chunks):
    col_tiles = cell_count // LANE
    per = col_tiles // chunks
    main_cols = per * chunks * LANE
    full_rows = (time_count // ROW_TILE) * ROW_TILE
    rest_rows = (time_count - full_rows) * (main_cols // LANE)
    rest_rows += time_count * (-(-(cell_count - main_cols) // LANE))
    share = -(-rest_rows // chunks)
    rows = per * full_rows + share
    padded_rows = -(-rows // ROW_TILE) * ROW_TILE
    return per, main_cols, full_rows, share, padded_rows - rows


def rest_chunks(low, right, chunks, share):
    parts = []
    if low.shape[0]:
        height = low.shape[0]
        parts.append(low.reshape(height, -1, LANE).transpose(1, 0, 2).reshape(-1, LANE))
    if right.shape[1]:
        height, width = right.shape
        tiles = -(-width // LANE)
        right = jnp.pad(right, ((0, 0), (0, tiles * LANE - width)))
        parts.append(right.reshape(height, tiles, LANE).transpose(1, 0, 2).reshape(-1, LANE))
    rest = jnp.concatenate(parts, axis=0)
    rest = jnp.pad(rest, ((0, share * chunks - rest.shape[0]), (0, 0)))
    return rest.reshape(chunks, share, LANE)


def assemble(main, rest, extra, chunks, dtype):
    pieces = [main, rest]
    if extra:
        pieces.append(jnp.zeros((chunks, extra, LANE), dtype))
    return jnp.concatenate(pieces, axis=1)


def pack_kernel(full_rows, per, share, values_ref, out_ref, rest_ref):
    time_count, cell_count = values_ref.shape
    chunks, rows, _ = out_ref.shape
    main_tiles = chunks * per
    main_cols = main_tiles * LANE
    for k in range(chunks):
        for q in range(per):
            j = k * per + q
            out_ref[k, q * full_rows:(q + 1) * full_rows, :] = values_ref[0:full_rows, j * LANE:(j + 1) * LANE]
    rest_ref[...] = jnp.zeros(rest_ref.shape, rest_ref.dtype)
    low = time_count - full_rows
    at = 0
    if low:
        for j in range(main_tiles):
            rest_ref[at:at + low, :] = values_ref[full_rows:time_count, j * LANE:(j + 1) * LANE].astype(jnp.float32)
            at += low
    for lo in range(main_cols, cell_count, LANE):
        width = min(LANE, cell_count - lo)
        rest_ref[at:at + time_count, 0:width] = values_ref[:, lo:lo + width].astype(jnp.float32)
        at += time_count
    for k in range(chunks):
        out_ref[k, per * full_rows:per * full_rows + share, :] = rest_ref[k * share:(k + 1) * share, :].astype(out_ref.dtype)
        if rows > per * full_rows + share:
            out_ref[k, per * full_rows + share:, :] = jnp.zeros((rows - per * full_rows - share, LANE), out_ref.dtype)


def dense_chunks(values, chunks):
    time_count, cell_count = values.shape
    per, main_cols, full_rows, share, extra = layout_of(time_count, cell_count, chunks)
    rows = per * full_rows + share + extra
    return pl.pallas_call(
        functools.partial(pack_kernel, full_rows, per, share),
        out_shape=jax.ShapeDtypeStruct((chunks, rows, LANE), values.dtype),
        in_specs=[pl.BlockSpec(memory_space=pltpu.VMEM)],
        out_specs=pl.BlockSpec(memory_space=pltpu.VMEM),
        scratch_shapes=[pltpu.VMEM((share * chunks, LANE), jnp.float32)],
        cost_estimate=pl.CostEstimate(flops=0, transcendentals=0, bytes_accessed=4 * chunks * rows * LANE),
    )(values)


def weighted_dense_chunks(footprint, time_cov, lat_cov, lon_cov, chunks):
    time_count, cell_count = footprint.shape
    lat_count = lat_cov.shape[0]
    lon_count = lon_cov.shape[0]
    per, main_cols, full_rows, share, extra = layout_of(time_count, cell_count, chunks)
    along_lon = jnp.dot(
        footprint.reshape(time_count * lat_count, lon_count),
        lon_cov,
        preferred_element_type=jnp.float32,
    ).astype(jnp.bfloat16)
    along_lat = jnp.einsum(
        "tab,ac->tcb",
        along_lon.reshape(time_count, lat_count, lon_count),
        lat_cov,
        preferred_element_type=jnp.float32,
    ).astype(jnp.bfloat16)
    along_lat = along_lat.reshape(time_count, cell_count)
    main = along_lat[:, :main_cols].reshape(time_count, chunks * per, LANE)
    main = jnp.einsum("ts,tjl->jsl", time_cov[:, :full_rows], main, preferred_element_type=jnp.float32)
    main = main.astype(jnp.bfloat16).reshape(chunks, per * full_rows, LANE)
    low = jnp.dot(time_cov[:, full_rows:].T, along_lat[:, :main_cols], preferred_element_type=jnp.float32)
    right = jnp.dot(time_cov.T, along_lat[:, main_cols:], preferred_element_type=jnp.float32)
    rest = rest_chunks(low.astype(jnp.bfloat16), right.astype(jnp.bfloat16), chunks, share)
    return assemble(main, rest, extra, chunks, jnp.bfloat16)


def local(footprints, time_cov, lat_cov, lon_cov):
    space_count = lax.axis_size("space")
    rec_count = lax.axis_size("rec")
    rec_index = lax.axis_index("rec")
    plain = dense_chunks(footprints[0], space_count)
    plain, footprint = lax.optimization_barrier((plain, footprints[0]))
    plain_here = lax.all_to_all(plain, "space", split_axis=0, concat_axis=0, tiled=True)
    weighted = weighted_dense_chunks(footprint, time_cov, lat_cov, lon_cov, space_count)
    weighted_here = lax.all_to_all(weighted, "space", split_axis=0, concat_axis=0, tiled=True)
    contract = (((1, 2), (1, 2)), ((), ()))
    group = plain_here.shape[0]
    received = [plain_here]
    for shift in range(1, rec_count):
        perm = [(i, (i + shift) % rec_count) for i in range(rec_count)]
        received.append(lax.ppermute(plain_here, "rec", perm))
    ordered = []
    for g in range(rec_count):
        choice = received[0]
        for shift in range(1, rec_count):
            choice = jnp.where((rec_index + rec_count - shift) % rec_count == g, received[shift], choice)
        ordered.append(choice)
    everyone = jnp.concatenate(ordered, axis=0)
    partial_value = lax.dot_general(weighted_here, everyone, contract, preferred_element_type=jnp.float32)
    spread = lax.all_to_all(partial_value, "space", split_axis=0, concat_axis=0, tiled=True)
    return jnp.sum(spread, axis=0, keepdims=True)


def solution(mesh):
    in_specs = (P(("rec", "space"), None, None), P(), P(), P())
    out_specs = P(("rec", "space"), None)
    return jax.shard_map(local, mesh=mesh, in_specs=in_specs, out_specs=out_specs, check_vma=False)
```

```python
import functools
import jax
import jax.numpy as jnp
from jax import lax
from jax.sharding import PartitionSpec as P
from jax.experimental import pallas as pl
from jax.experimental.pallas import tpu as pltpu

ROW_TILE = 16
LANE = 128


def layout_of(time_count, cell_count, chunks):
    col_tiles = cell_count // LANE
    per = col_tiles // chunks
    main_cols = per * chunks * LANE
    full_rows = (time_count // ROW_TILE) * ROW_TILE
    rest_rows = (time_count - full_rows) * (main_cols // LANE)
    rest_rows += time_count * (-(-(cell_count - main_cols) // LANE))
    share = -(-rest_rows // chunks)
    rows = per * full_rows + share
    padded_rows = -(-rows // ROW_TILE) * ROW_TILE
    return per, main_cols, full_rows, share, padded_rows - rows


def rest_chunks(low, right, chunks, share):
    parts = []
    if low.shape[0]:
        height = low.shape[0]
        parts.append(low.reshape(height, -1, LANE).transpose(1, 0, 2).reshape(-1, LANE))
    if right.shape[1]:
        height, width = right.shape
        tiles = -(-width // LANE)
        right = jnp.pad(right, ((0, 0), (0, tiles * LANE - width)))
        parts.append(right.reshape(height, tiles, LANE).transpose(1, 0, 2).reshape(-1, LANE))
    rest = jnp.concatenate(parts, axis=0)
    rest = jnp.pad(rest, ((0, share * chunks - rest.shape[0]), (0, 0)))
    return rest.reshape(chunks, share, LANE)


def assemble(main, rest, extra, chunks, dtype):
    pieces = [main, rest]
    if extra:
        pieces.append(jnp.zeros((chunks, extra, LANE), dtype))
    return jnp.concatenate(pieces, axis=1)


def pack_kernel(full_rows, per, share, values_ref, out_ref, rest_ref):
    time_count, cell_count = values_ref.shape
    chunks, rows, _ = out_ref.shape
    main_tiles = chunks * per
    main_cols = main_tiles * LANE
    for k in range(chunks):
        for q in range(per):
            j = k * per + q
            out_ref[k, q * full_rows:(q + 1) * full_rows, :] = values_ref[0:full_rows, j * LANE:(j + 1) * LANE]
    rest_ref[...] = jnp.zeros(rest_ref.shape, rest_ref.dtype)
    low = time_count - full_rows
    at = 0
    if low:
        for j in range(main_tiles):
            rest_ref[at:at + low, :] = values_ref[full_rows:time_count, j * LANE:(j + 1) * LANE].astype(jnp.float32)
            at += low
    for lo in range(main_cols, cell_count, LANE):
        width = min(LANE, cell_count - lo)
        rest_ref[at:at + time_count, 0:width] = values_ref[:, lo:lo + width].astype(jnp.float32)
        at += time_count
    for k in range(chunks):
        out_ref[k, per * full_rows:per * full_rows + share, :] = rest_ref[k * share:(k + 1) * share, :].astype(out_ref.dtype)
        if rows > per * full_rows + share:
            out_ref[k, per * full_rows + share:, :] = jnp.zeros((rows - per * full_rows - share, LANE), out_ref.dtype)


def dense_chunks(values, chunks):
    time_count, cell_count = values.shape
    per, main_cols, full_rows, share, extra = layout_of(time_count, cell_count, chunks)
    rows = per * full_rows + share + extra
    return pl.pallas_call(
        functools.partial(pack_kernel, full_rows, per, share),
        out_shape=jax.ShapeDtypeStruct((chunks, rows, LANE), values.dtype),
        in_specs=[pl.BlockSpec(memory_space=pltpu.VMEM)],
        out_specs=pl.BlockSpec(memory_space=pltpu.VMEM),
        scratch_shapes=[pltpu.VMEM((share * chunks, LANE), jnp.float32)],
        cost_estimate=pl.CostEstimate(flops=0, transcendentals=0, bytes_accessed=4 * chunks * rows * LANE),
    )(values)


def weighted_dense_chunks(footprint, time_cov, lat_cov, lon_cov, chunks):
    time_count, cell_count = footprint.shape
    lat_count = lat_cov.shape[0]
    lon_count = lon_cov.shape[0]
    per, main_cols, full_rows, share, extra = layout_of(time_count, cell_count, chunks)
    along_lon = jnp.dot(
        footprint.reshape(time_count * lat_count, lon_count),
        lon_cov,
        preferred_element_type=jnp.float32,
    ).astype(jnp.bfloat16)
    along_lat = jnp.einsum(
        "tab,ac->tcb",
        along_lon.reshape(time_count, lat_count, lon_count),
        lat_cov,
        preferred_element_type=jnp.float32,
    ).astype(jnp.bfloat16)
    along_lat = along_lat.reshape(time_count, cell_count)
    main = along_lat[:, :main_cols].reshape(time_count, chunks * per, LANE)
    main = jnp.einsum("ts,tjl->jsl", time_cov[:, :full_rows], main, preferred_element_type=jnp.float32)
    main = main.astype(jnp.bfloat16).reshape(chunks, per * full_rows, LANE)
    low = jnp.dot(time_cov[:, full_rows:].T, along_lat[:, :main_cols], preferred_element_type=jnp.float32)
    right = jnp.dot(time_cov.T, along_lat[:, main_cols:], preferred_element_type=jnp.float32)
    rest = rest_chunks(low.astype(jnp.bfloat16), right.astype(jnp.bfloat16), chunks, share)
    return assemble(main, rest, extra, chunks, jnp.bfloat16)


def local(footprints, time_cov, lat_cov, lon_cov):
    space_count = lax.axis_size("space")
    rec_count = lax.axis_size("rec")
    rec_index = lax.axis_index("rec")
    plain = dense_chunks(footprints[0], space_count)
    plain, footprint = lax.optimization_barrier((plain, footprints[0]))
    space_index = lax.axis_index("space")
    shifted = [lax.dynamic_index_in_dim(plain, space_index, 0, keepdims=True)]
    for shift in range(1, space_count):
        perm = [(i, (i + shift) % space_count) for i in range(space_count)]
        piece = lax.dynamic_index_in_dim(plain, (space_index + shift) % space_count, 0, keepdims=True)
        shifted.append(lax.ppermute(piece, "space", perm))
    plain_here = jnp.concatenate(shifted, axis=0)
    weighted = weighted_dense_chunks(footprint, time_cov, lat_cov, lon_cov, space_count)
    weighted_here = lax.all_to_all(weighted, "space", split_axis=0, concat_axis=0, tiled=True)
    contract = (((1, 2), (1, 2)), ((), ()))
    group = plain_here.shape[0]
    received = [plain_here]
    for shift in range(1, rec_count):
        perm = [(i, (i + shift) % rec_count) for i in range(rec_count)]
        received.append(lax.ppermute(plain_here, "rec", perm))
    ordered = []
    for g in range(rec_count):
        choice = received[0]
        for shift in range(1, rec_count):
            choice = jnp.where((rec_index + rec_count - shift) % rec_count == g, received[shift], choice)
        ordered.append(choice)
    everyone = jnp.concatenate(ordered, axis=0)
    partial_value = lax.dot_general(weighted_here, everyone, contract, preferred_element_type=jnp.float32)
    source = (space_index - jnp.arange(group)) % group
    partial_value = jnp.take(partial_value.reshape(group, rec_count, group), source, axis=2).reshape(group, rec_count * group)
    spread = lax.all_to_all(partial_value, "space", split_axis=0, concat_axis=0, tiled=True)
    return jnp.sum(spread, axis=0, keepdims=True)


def solution(mesh):
    in_specs = (P(("rec", "space"), None, None), P(), P(), P())
    out_specs = P(("rec", "space"), None)
    return jax.shard_map(local, mesh=mesh, in_specs=in_specs, out_specs=out_specs, check_vma=False)
```

```python
import functools
import jax
import jax.numpy as jnp
from jax import lax
from jax.sharding import PartitionSpec as P
from jax.experimental import pallas as pl
from jax.experimental.pallas import tpu as pltpu

ROW_TILE = 16
LANE = 128


def layout_of(time_count, cell_count, chunks):
    col_tiles = cell_count // LANE
    per = col_tiles // chunks
    main_cols = per * chunks * LANE
    full_rows = (time_count // ROW_TILE) * ROW_TILE
    rest_rows = (time_count - full_rows) * (main_cols // LANE)
    rest_rows += time_count * (-(-(cell_count - main_cols) // LANE))
    share = -(-rest_rows // chunks)
    rows = per * full_rows + share
    padded_rows = -(-rows // ROW_TILE) * ROW_TILE
    return per, main_cols, full_rows, share, padded_rows - rows


def rest_chunks(low, right, chunks, share):
    parts = []
    if low.shape[0]:
        height = low.shape[0]
        parts.append(low.reshape(height, -1, LANE).transpose(1, 0, 2).reshape(-1, LANE))
    if right.shape[1]:
        height, width = right.shape
        tiles = -(-width // LANE)
        right = jnp.pad(right, ((0, 0), (0, tiles * LANE - width)))
        parts.append(right.reshape(height, tiles, LANE).transpose(1, 0, 2).reshape(-1, LANE))
    rest = jnp.concatenate(parts, axis=0)
    rest = jnp.pad(rest, ((0, share * chunks - rest.shape[0]), (0, 0)))
    return rest.reshape(chunks, share, LANE)


def assemble(main, rest, extra, chunks, dtype):
    pieces = [main, rest]
    if extra:
        pieces.append(jnp.zeros((chunks, extra, LANE), dtype))
    return jnp.concatenate(pieces, axis=1)


def pack_kernel(full_rows, per, share, values_ref, out_ref, rest_ref, sems):
    time_count, cell_count = values_ref.shape
    chunks, rows, _ = out_ref.shape
    main_tiles = chunks * per
    main_cols = main_tiles * LANE
    copies = []
    for k in range(chunks):
        for q in range(per):
            j = k * per + q
            copy = pltpu.make_async_copy(
                values_ref.at[0:full_rows, j * LANE:(j + 1) * LANE],
                out_ref.at[k, q * full_rows:(q + 1) * full_rows, :],
                sems.at[j],
            )
            copy.start()
            copies.append(copy)
    rest_ref[...] = jnp.zeros(rest_ref.shape, rest_ref.dtype)
    low = time_count - full_rows
    at = 0
    if low:
        for j in range(main_tiles):
            rest_ref[at:at + low, :] = values_ref[full_rows:time_count, j * LANE:(j + 1) * LANE].astype(jnp.float32)
            at += low
    for lo in range(main_cols, cell_count, LANE):
        width = min(LANE, cell_count - lo)
        rest_ref[at:at + time_count, 0:width] = values_ref[:, lo:lo + width].astype(jnp.float32)
        at += time_count
    for k in range(chunks):
        out_ref[k, per * full_rows:per * full_rows + share, :] = rest_ref[k * share:(k + 1) * share, :].astype(out_ref.dtype)
        if rows > per * full_rows + share:
            out_ref[k, per * full_rows + share:, :] = jnp.zeros((rows - per * full_rows - share, LANE), out_ref.dtype)
    for copy in copies:
        copy.wait()


def dense_chunks(values, chunks):
    time_count, cell_count = values.shape
    per, main_cols, full_rows, share, extra = layout_of(time_count, cell_count, chunks)
    rows = per * full_rows + share + extra
    return pl.pallas_call(
        functools.partial(pack_kernel, full_rows, per, share),
        out_shape=jax.ShapeDtypeStruct((chunks, rows, LANE), values.dtype),
        in_specs=[pl.BlockSpec(memory_space=pltpu.VMEM)],
        out_specs=pl.BlockSpec(memory_space=pltpu.VMEM),
        scratch_shapes=[pltpu.VMEM((share * chunks, LANE), jnp.float32), pltpu.SemaphoreType.DMA((chunks * per,))],
        cost_estimate=pl.CostEstimate(flops=0, transcendentals=0, bytes_accessed=4 * chunks * rows * LANE),
    )(values)


def weighted_dense_chunks(footprint, time_cov, lat_cov, lon_cov, chunks):
    time_count, cell_count = footprint.shape
    lat_count = lat_cov.shape[0]
    lon_count = lon_cov.shape[0]
    per, main_cols, full_rows, share, extra = layout_of(time_count, cell_count, chunks)
    along_lon = jnp.dot(
        footprint.reshape(time_count * lat_count, lon_count),
        lon_cov,
        preferred_element_type=jnp.float32,
    ).astype(jnp.bfloat16)
    along_lat = jnp.einsum(
        "tab,ac->tcb",
        along_lon.reshape(time_count, lat_count, lon_count),
        lat_cov,
        preferred_element_type=jnp.float32,
    ).astype(jnp.bfloat16)
    along_lat = along_lat.reshape(time_count, cell_count)
    main = along_lat[:, :main_cols].reshape(time_count, chunks * per, LANE)
    main = jnp.einsum("ts,tjl->jsl", time_cov[:, :full_rows], main, preferred_element_type=jnp.float32)
    main = main.astype(jnp.bfloat16).reshape(chunks, per * full_rows, LANE)
    low = jnp.dot(time_cov[:, full_rows:].T, along_lat[:, :main_cols], preferred_element_type=jnp.float32)
    right = jnp.dot(time_cov.T, along_lat[:, main_cols:], preferred_element_type=jnp.float32)
    rest = rest_chunks(low.astype(jnp.bfloat16), right.astype(jnp.bfloat16), chunks, share)
    return assemble(main, rest, extra, chunks, jnp.bfloat16)


def local(footprints, time_cov, lat_cov, lon_cov):
    space_count = lax.axis_size("space")
    rec_count = lax.axis_size("rec")
    rec_index = lax.axis_index("rec")
    plain = dense_chunks(footprints[0], space_count)
    plain, footprint = lax.optimization_barrier((plain, footprints[0]))
    plain_here = lax.all_to_all(plain, "space", split_axis=0, concat_axis=0, tiled=True)
    weighted = weighted_dense_chunks(footprint, time_cov, lat_cov, lon_cov, space_count)
    weighted_here = lax.all_to_all(weighted, "space", split_axis=0, concat_axis=0, tiled=True)
    contract = (((1, 2), (1, 2)), ((), ()))
    group = plain_here.shape[0]
    received = [plain_here]
    for shift in range(1, rec_count):
        perm = [(i, (i + shift) % rec_count) for i in range(rec_count)]
        received.append(lax.ppermute(plain_here, "rec", perm))
    ordered = []
    for g in range(rec_count):
        choice = received[0]
        for shift in range(1, rec_count):
            choice = jnp.where((rec_index + rec_count - shift) % rec_count == g, received[shift], choice)
        ordered.append(choice)
    everyone = jnp.concatenate(ordered, axis=0)
    partial_value = lax.dot_general(weighted_here, everyone, contract, preferred_element_type=jnp.float32)
    spread = lax.all_to_all(partial_value, "space", split_axis=0, concat_axis=0, tiled=True)
    return jnp.sum(spread, axis=0, keepdims=True)


def solution(mesh):
    in_specs = (P(("rec", "space"), None, None), P(), P(), P())
    out_specs = P(("rec", "space"), None)
    return jax.shard_map(local, mesh=mesh, in_specs=in_specs, out_specs=out_specs, check_vma=False)
```

```python
import functools
import jax
import jax.numpy as jnp
from jax import lax
from jax.sharding import PartitionSpec as P
from jax.experimental import pallas as pl
from jax.experimental.pallas import tpu as pltpu

ROW_TILE = 16
LANE = 128


def layout_of(time_count, cell_count, chunks):
    col_tiles = cell_count // LANE
    per = col_tiles // chunks
    main_cols = per * chunks * LANE
    full_rows = (time_count // ROW_TILE) * ROW_TILE
    rest_rows = (time_count - full_rows) * (main_cols // LANE)
    rest_rows += time_count * (-(-(cell_count - main_cols) // LANE))
    share = -(-rest_rows // chunks)
    rows = per * full_rows + share
    padded_rows = -(-rows // ROW_TILE) * ROW_TILE
    return per, main_cols, full_rows, share, padded_rows - rows


def rest_chunks(low, right, chunks, share):
    parts = []
    if low.shape[0]:
        height = low.shape[0]
        parts.append(low.reshape(height, -1, LANE).transpose(1, 0, 2).reshape(-1, LANE))
    if right.shape[1]:
        height, width = right.shape
        tiles = -(-width // LANE)
        right = jnp.pad(right, ((0, 0), (0, tiles * LANE - width)))
        parts.append(right.reshape(height, tiles, LANE).transpose(1, 0, 2).reshape(-1, LANE))
    rest = jnp.concatenate(parts, axis=0)
    rest = jnp.pad(rest, ((0, share * chunks - rest.shape[0]), (0, 0)))
    return rest.reshape(chunks, share, LANE)


def assemble(main, rest, extra, chunks, dtype):
    pieces = [main, rest]
    if extra:
        pieces.append(jnp.zeros((chunks, extra, LANE), dtype))
    return jnp.concatenate(pieces, axis=1)


def pack_kernel(full_rows, per, share, values_hbm, out_hbm, values, main_out, rest_out, rest_ref, in_sems, out_sems):
    time_count, cell_count = values.shape
    chunks, rows, _ = out_hbm.shape
    main_tiles = chunks * per
    main_cols = main_tiles * LANE
    groups = 4 if chunks % 4 == 0 else 1
    width = main_cols // groups
    loads = []
    for g in range(groups):
        load = pltpu.make_async_copy(
            values_hbm.at[:, g * width:(g + 1) * width], values.at[:, g * width:(g + 1) * width], in_sems.at[g]
        )
        load.start()
        loads.append(load)
    if cell_count > main_cols:
        tail = pltpu.make_async_copy(
            values_hbm.at[:, main_cols:cell_count], values.at[:, main_cols:cell_count], in_sems.at[groups]
        )
        tail.start()
        loads.append(tail)
    stores = []
    per_group = chunks // groups
    for g in range(groups):
        loads[g].wait()
        for k in range(g * per_group, (g + 1) * per_group):
            for q in range(per):
                j = k * per + q
                main_out[k, q * full_rows:(q + 1) * full_rows, :] = values[0:full_rows, j * LANE:(j + 1) * LANE]
        store = pltpu.make_async_copy(
            main_out.at[g * per_group:(g + 1) * per_group],
            out_hbm.at[g * per_group:(g + 1) * per_group, 0:per * full_rows, :],
            out_sems.at[g],
        )
        store.start()
        stores.append(store)
    if cell_count > main_cols:
        loads[groups].wait()
    rest_ref[...] = jnp.zeros(rest_ref.shape, rest_ref.dtype)
    low = time_count - full_rows
    at = 0
    if low:
        for j in range(main_tiles):
            rest_ref[at:at + low, :] = values[full_rows:time_count, j * LANE:(j + 1) * LANE].astype(jnp.float32)
            at += low
    for lo in range(main_cols, cell_count, LANE):
        span = min(LANE, cell_count - lo)
        rest_ref[at:at + time_count, 0:span] = values[:, lo:lo + span].astype(jnp.float32)
        at += time_count
    tail_rows = rows - per * full_rows
    for k in range(chunks):
        rest_out[k, 0:share, :] = rest_ref[k * share:(k + 1) * share, :].astype(rest_out.dtype)
        if tail_rows > share:
            rest_out[k, share:, :] = jnp.zeros((tail_rows - share, LANE), rest_out.dtype)
    last = pltpu.make_async_copy(rest_out, out_hbm.at[:, per * full_rows:rows, :], out_sems.at[groups])
    last.start()
    for store in stores:
        store.wait()
    last.wait()


def dense_chunks(values, chunks):
    time_count, cell_count = values.shape
    per, main_cols, full_rows, share, extra = layout_of(time_count, cell_count, chunks)
    rows = per * full_rows + share + extra
    return pl.pallas_call(
        functools.partial(pack_kernel, full_rows, per, share),
        out_shape=jax.ShapeDtypeStruct((chunks, rows, LANE), values.dtype),
        in_specs=[pl.BlockSpec(memory_space=pl.ANY)],
        out_specs=pl.BlockSpec(memory_space=pl.ANY),
        scratch_shapes=[
            pltpu.VMEM((time_count, cell_count), values.dtype),
            pltpu.VMEM((chunks, per * full_rows, LANE), values.dtype),
            pltpu.VMEM((chunks, rows - per * full_rows, LANE), values.dtype),
            pltpu.VMEM((share * chunks, LANE), jnp.float32),
            pltpu.SemaphoreType.DMA((5,)),
            pltpu.SemaphoreType.DMA((5,)),
        ],
        cost_estimate=pl.CostEstimate(flops=0, transcendentals=0, bytes_accessed=4 * chunks * rows * LANE),
    )(values)


def weighted_dense_chunks(footprint, time_cov, lat_cov, lon_cov, chunks):
    time_count, cell_count = footprint.shape
    lat_count = lat_cov.shape[0]
    lon_count = lon_cov.shape[0]
    per, main_cols, full_rows, share, extra = layout_of(time_count, cell_count, chunks)
    along_lon = jnp.dot(
        footprint.reshape(time_count * lat_count, lon_count),
        lon_cov,
        preferred_element_type=jnp.float32,
    ).astype(jnp.bfloat16)
    along_lat = jnp.einsum(
        "tab,ac->tcb",
        along_lon.reshape(time_count, lat_count, lon_count),
        lat_cov,
        preferred_element_type=jnp.float32,
    ).astype(jnp.bfloat16)
    along_lat = along_lat.reshape(time_count, cell_count)
    main = along_lat[:, :main_cols].reshape(time_count, chunks * per, LANE)
    main = jnp.einsum("ts,tjl->jsl", time_cov[:, :full_rows], main, preferred_element_type=jnp.float32)
    main = main.astype(jnp.bfloat16).reshape(chunks, per * full_rows, LANE)
    low = jnp.dot(time_cov[:, full_rows:].T, along_lat[:, :main_cols], preferred_element_type=jnp.float32)
    right = jnp.dot(time_cov.T, along_lat[:, main_cols:], preferred_element_type=jnp.float32)
    rest = rest_chunks(low.astype(jnp.bfloat16), right.astype(jnp.bfloat16), chunks, share)
    return assemble(main, rest, extra, chunks, jnp.bfloat16)


def local(footprints, time_cov, lat_cov, lon_cov):
    space_count = lax.axis_size("space")
    rec_count = lax.axis_size("rec")
    rec_index = lax.axis_index("rec")
    plain = dense_chunks(footprints[0], space_count)
    plain, footprint = lax.optimization_barrier((plain, footprints[0]))
    plain_here = lax.all_to_all(plain, "space", split_axis=0, concat_axis=0, tiled=True)
    weighted = weighted_dense_chunks(footprint, time_cov, lat_cov, lon_cov, space_count)
    weighted_here = lax.all_to_all(weighted, "space", split_axis=0, concat_axis=0, tiled=True)
    contract = (((1, 2), (1, 2)), ((), ()))
    group = plain_here.shape[0]
    received = [plain_here]
    for shift in range(1, rec_count):
        perm = [(i, (i + shift) % rec_count) for i in range(rec_count)]
        received.append(lax.ppermute(plain_here, "rec", perm))
    ordered = []
    for g in range(rec_count):
        choice = received[0]
        for shift in range(1, rec_count):
            choice = jnp.where((rec_index + rec_count - shift) % rec_count == g, received[shift], choice)
        ordered.append(choice)
    everyone = jnp.concatenate(ordered, axis=0)
    partial_value = lax.dot_general(weighted_here, everyone, contract, preferred_element_type=jnp.float32)
    spread = lax.all_to_all(partial_value, "space", split_axis=0, concat_axis=0, tiled=True)
    return jnp.sum(spread, axis=0, keepdims=True)


def solution(mesh):
    in_specs = (P(("rec", "space"), None, None), P(), P(), P())
    out_specs = P(("rec", "space"), None)
    return jax.shard_map(local, mesh=mesh, in_specs=in_specs, out_specs=out_specs, check_vma=False)
```

```python
import functools
import jax
import jax.numpy as jnp
from jax import lax
from jax.sharding import PartitionSpec as P
from jax.experimental import pallas as pl
from jax.experimental.pallas import tpu as pltpu

ROW_TILE = 16
LANE = 128


def layout_of(time_count, cell_count, chunks):
    col_tiles = cell_count // LANE
    per = col_tiles // chunks
    main_cols = per * chunks * LANE
    full_rows = (time_count // ROW_TILE) * ROW_TILE
    rest_rows = (time_count - full_rows) * (main_cols // LANE)
    rest_rows += time_count * (-(-(cell_count - main_cols) // LANE))
    share = -(-rest_rows // chunks)
    rows = per * full_rows + share
    padded_rows = -(-rows // ROW_TILE) * ROW_TILE
    return per, main_cols, full_rows, share, padded_rows - rows


def rest_chunks(low, right, chunks, share):
    parts = []
    if low.shape[0]:
        height = low.shape[0]
        parts.append(low.reshape(height, -1, LANE).transpose(1, 0, 2).reshape(-1, LANE))
    if right.shape[1]:
        height, width = right.shape
        tiles = -(-width // LANE)
        right = jnp.pad(right, ((0, 0), (0, tiles * LANE - width)))
        parts.append(right.reshape(height, tiles, LANE).transpose(1, 0, 2).reshape(-1, LANE))
    rest = jnp.concatenate(parts, axis=0)
    rest = jnp.pad(rest, ((0, share * chunks - rest.shape[0]), (0, 0)))
    return rest.reshape(chunks, share, LANE)


def assemble(main, rest, extra, chunks, dtype):
    pieces = [main, rest]
    if extra:
        pieces.append(jnp.zeros((chunks, extra, LANE), dtype))
    return jnp.concatenate(pieces, axis=1)


def pack_kernel(full_rows, per, share, values_hbm, out_hbm, values, main_out, rest_out, rest_ref, in_sems, out_sems):
    time_count, cell_count = values.shape
    chunks, rows, _ = out_hbm.shape
    main_tiles = chunks * per
    main_cols = main_tiles * LANE
    groups = 8 if chunks % 8 == 0 else 1
    width = main_cols // groups
    loads = []
    for g in range(groups):
        load = pltpu.make_async_copy(
            values_hbm.at[:, g * width:(g + 1) * width], values.at[:, g * width:(g + 1) * width], in_sems.at[g]
        )
        load.start()
        loads.append(load)
    if cell_count > main_cols:
        tail = pltpu.make_async_copy(
            values_hbm.at[:, main_cols:cell_count], values.at[:, main_cols:cell_count], in_sems.at[groups]
        )
        tail.start()
        loads.append(tail)
    stores = []
    per_group = chunks // groups
    rest_ref[...] = jnp.zeros(rest_ref.shape, rest_ref.dtype)
    low = time_count - full_rows
    for g in range(groups):
        loads[g].wait()
        for k in range(g * per_group, (g + 1) * per_group):
            for q in range(per):
                j = k * per + q
                main_out[k, q * full_rows:(q + 1) * full_rows, :] = values[0:full_rows, j * LANE:(j + 1) * LANE]
                if low:
                    rest_ref[j * low:(j + 1) * low, :] = values[full_rows:time_count, j * LANE:(j + 1) * LANE].astype(jnp.float32)
        store = pltpu.make_async_copy(
            main_out.at[g * per_group:(g + 1) * per_group],
            out_hbm.at[g * per_group:(g + 1) * per_group, 0:per * full_rows, :],
            out_sems.at[g],
        )
        store.start()
        stores.append(store)
    if cell_count > main_cols:
        loads[groups].wait()
    at = low * main_tiles
    for lo in range(main_cols, cell_count, LANE):
        span = min(LANE, cell_count - lo)
        rest_ref[at:at + time_count, 0:span] = values[:, lo:lo + span].astype(jnp.float32)
        at += time_count
    tail_rows = rows - per * full_rows
    for k in range(chunks):
        rest_out[k, 0:share, :] = rest_ref[k * share:(k + 1) * share, :].astype(rest_out.dtype)
        if tail_rows > share:
            rest_out[k, share:, :] = jnp.zeros((tail_rows - share, LANE), rest_out.dtype)
    last = pltpu.make_async_copy(rest_out, out_hbm.at[:, per * full_rows:rows, :], out_sems.at[groups])
    last.start()
    for store in stores:
        store.wait()
    last.wait()


def dense_chunks(values, chunks):
    time_count, cell_count = values.shape
    per, main_cols, full_rows, share, extra = layout_of(time_count, cell_count, chunks)
    rows = per * full_rows + share + extra
    return pl.pallas_call(
        functools.partial(pack_kernel, full_rows, per, share),
        out_shape=jax.ShapeDtypeStruct((chunks, rows, LANE), values.dtype),
        in_specs=[pl.BlockSpec(memory_space=pl.ANY)],
        out_specs=pl.BlockSpec(memory_space=pl.ANY),
        scratch_shapes=[
            pltpu.VMEM((time_count, cell_count), values.dtype),
            pltpu.VMEM((chunks, per * full_rows, LANE), values.dtype),
            pltpu.VMEM((chunks, rows - per * full_rows, LANE), values.dtype),
            pltpu.VMEM((share * chunks, LANE), jnp.float32),
            pltpu.SemaphoreType.DMA((9,)),
            pltpu.SemaphoreType.DMA((9,)),
        ],
        cost_estimate=pl.CostEstimate(flops=0, transcendentals=0, bytes_accessed=4 * chunks * rows * LANE),
    )(values)


def weighted_dense_chunks(footprint, time_cov, lat_cov, lon_cov, chunks):
    time_count, cell_count = footprint.shape
    lat_count = lat_cov.shape[0]
    lon_count = lon_cov.shape[0]
    per, main_cols, full_rows, share, extra = layout_of(time_count, cell_count, chunks)
    along_lon = jnp.dot(
        footprint.reshape(time_count * lat_count, lon_count),
        lon_cov,
        preferred_element_type=jnp.float32,
    ).astype(jnp.bfloat16)
    along_lat = jnp.einsum(
        "tab,ac->tcb",
        along_lon.reshape(time_count, lat_count, lon_count),
        lat_cov,
        preferred_element_type=jnp.float32,
    ).astype(jnp.bfloat16)
    along_lat = along_lat.reshape(time_count, cell_count)
    main = along_lat[:, :main_cols].reshape(time_count, chunks * per, LANE)
    main = jnp.einsum("ts,tjl->jsl", time_cov[:, :full_rows], main, preferred_element_type=jnp.float32)
    main = main.astype(jnp.bfloat16).reshape(chunks, per * full_rows, LANE)
    low = jnp.dot(time_cov[:, full_rows:].T, along_lat[:, :main_cols], preferred_element_type=jnp.float32)
    right = jnp.dot(time_cov.T, along_lat[:, main_cols:], preferred_element_type=jnp.float32)
    rest = rest_chunks(low.astype(jnp.bfloat16), right.astype(jnp.bfloat16), chunks, share)
    return assemble(main, rest, extra, chunks, jnp.bfloat16)


def local(footprints, time_cov, lat_cov, lon_cov):
    space_count = lax.axis_size("space")
    rec_count = lax.axis_size("rec")
    rec_index = lax.axis_index("rec")
    plain = dense_chunks(footprints[0], space_count)
    plain, footprint = lax.optimization_barrier((plain, footprints[0]))
    plain_here = lax.all_to_all(plain, "space", split_axis=0, concat_axis=0, tiled=True)
    weighted = weighted_dense_chunks(footprint, time_cov, lat_cov, lon_cov, space_count)
    weighted_here = lax.all_to_all(weighted, "space", split_axis=0, concat_axis=0, tiled=True)
    contract = (((1, 2), (1, 2)), ((), ()))
    group = plain_here.shape[0]
    received = [plain_here]
    for shift in range(1, rec_count):
        perm = [(i, (i + shift) % rec_count) for i in range(rec_count)]
        received.append(lax.ppermute(plain_here, "rec", perm))
    ordered = []
    for g in range(rec_count):
        choice = received[0]
        for shift in range(1, rec_count):
            choice = jnp.where((rec_index + rec_count - shift) % rec_count == g, received[shift], choice)
        ordered.append(choice)
    everyone = jnp.concatenate(ordered, axis=0)
    partial_value = lax.dot_general(weighted_here, everyone, contract, preferred_element_type=jnp.float32)
    spread = lax.all_to_all(partial_value, "space", split_axis=0, concat_axis=0, tiled=True)
    return jnp.sum(spread, axis=0, keepdims=True)


def solution(mesh):
    in_specs = (P(("rec", "space"), None, None), P(), P(), P())
    out_specs = P(("rec", "space"), None)
    return jax.shard_map(local, mesh=mesh, in_specs=in_specs, out_specs=out_specs, check_vma=False)
```

```python
import functools
import jax
import jax.numpy as jnp
from jax import lax
from jax.sharding import PartitionSpec as P
from jax.experimental import pallas as pl
from jax.experimental.pallas import tpu as pltpu

ROW_TILE = 16
LANE = 128


def layout_of(time_count, cell_count, chunks):
    col_tiles = cell_count // LANE
    per = col_tiles // chunks
    main_cols = per * chunks * LANE
    full_rows = (time_count // ROW_TILE) * ROW_TILE
    rest_rows = (time_count - full_rows) * (main_cols // LANE)
    rest_rows += time_count * (-(-(cell_count - main_cols) // LANE))
    share = -(-rest_rows // chunks)
    rows = per * full_rows + share
    padded_rows = -(-rows // ROW_TILE) * ROW_TILE
    return per, main_cols, full_rows, share, padded_rows - rows


def rest_chunks(low, right, chunks, share):
    parts = []
    if low.shape[0]:
        height = low.shape[0]
        parts.append(low.reshape(height, -1, LANE).transpose(1, 0, 2).reshape(-1, LANE))
    if right.shape[1]:
        height, width = right.shape
        tiles = -(-width // LANE)
        right = jnp.pad(right, ((0, 0), (0, tiles * LANE - width)))
        parts.append(right.reshape(height, tiles, LANE).transpose(1, 0, 2).reshape(-1, LANE))
    rest = jnp.concatenate(parts, axis=0)
    rest = jnp.pad(rest, ((0, share * chunks - rest.shape[0]), (0, 0)))
    return rest.reshape(chunks, share, LANE)


def assemble(main, rest, extra, chunks, dtype):
    pieces = [main, rest]
    if extra:
        pieces.append(jnp.zeros((chunks, extra, LANE), dtype))
    return jnp.concatenate(pieces, axis=1)


def pack_kernel(full_rows, per, share, values_hbm, out_hbm, values, main_out, rest_out, rest_ref, in_sems, out_sems):
    time_count, cell_count = values.shape
    chunks, rows, _ = out_hbm.shape
    main_tiles = chunks * per
    main_cols = main_tiles * LANE
    groups = 4 if chunks % 4 == 0 else 1
    width = main_cols // groups
    loads = []
    for g in range(groups):
        load = pltpu.make_async_copy(
            values_hbm.at[:, g * width:(g + 1) * width], values.at[:, g * width:(g + 1) * width], in_sems.at[g]
        )
        load.start()
        loads.append(load)
    if cell_count > main_cols:
        tail = pltpu.make_async_copy(
            values_hbm.at[:, main_cols:cell_count], values.at[:, main_cols:cell_count], in_sems.at[groups]
        )
        tail.start()
        loads.append(tail)
    stores = []
    per_group = chunks // groups
    for g in range(groups):
        loads[g].wait()
        for k in range(g * per_group, (g + 1) * per_group):
            for q in range(per):
                j = k * per + q
                main_out[k, q * full_rows:(q + 1) * full_rows, :] = values[0:full_rows, j * LANE:(j + 1) * LANE]
        store = pltpu.make_async_copy(
            main_out.at[g * per_group:(g + 1) * per_group],
            out_hbm.at[g * per_group:(g + 1) * per_group, 0:per * full_rows, :],
            out_sems.at[g],
        )
        store.start()
        stores.append(store)
    if cell_count > main_cols:
        loads[groups].wait()
    rest_ref[...] = jnp.zeros(rest_ref.shape, rest_ref.dtype)
    low = time_count - full_rows
    at = 0
    if low:
        for j in range(main_tiles):
            rest_ref[at:at + low, :] = values[full_rows:time_count, j * LANE:(j + 1) * LANE].astype(jnp.float32)
            at += low
    for lo in range(main_cols, cell_count, LANE):
        span = min(LANE, cell_count - lo)
        rest_ref[at:at + time_count, 0:span] = values[:, lo:lo + span].astype(jnp.float32)
        at += time_count
    tail_rows = rows - per * full_rows
    for k in range(chunks):
        rest_out[k, 0:share, :] = rest_ref[k * share:(k + 1) * share, :].astype(rest_out.dtype)
        if tail_rows > share:
            rest_out[k, share:, :] = jnp.zeros((tail_rows - share, LANE), rest_out.dtype)
    last = pltpu.make_async_copy(rest_out, out_hbm.at[:, per * full_rows:rows, :], out_sems.at[groups])
    last.start()
    for store in stores:
        store.wait()
    last.wait()


def dense_chunks(values, chunks):
    time_count, cell_count = values.shape
    per, main_cols, full_rows, share, extra = layout_of(time_count, cell_count, chunks)
    rows = per * full_rows + share + extra
    return pl.pallas_call(
        functools.partial(pack_kernel, full_rows, per, share),
        out_shape=jax.ShapeDtypeStruct((chunks, rows, LANE), values.dtype),
        in_specs=[pl.BlockSpec(memory_space=pl.ANY)],
        out_specs=pl.BlockSpec(memory_space=pl.ANY),
        scratch_shapes=[
            pltpu.VMEM((time_count, cell_count), values.dtype),
            pltpu.VMEM((chunks, per * full_rows, LANE), values.dtype),
            pltpu.VMEM((chunks, rows - per * full_rows, LANE), values.dtype),
            pltpu.VMEM((share * chunks, LANE), jnp.float32),
            pltpu.SemaphoreType.DMA((5,)),
            pltpu.SemaphoreType.DMA((5,)),
        ],
        cost_estimate=pl.CostEstimate(flops=0, transcendentals=0, bytes_accessed=4 * chunks * rows * LANE),
    )(values)


def weighted_dense_chunks(footprint, time_cov, lat_cov, lon_cov, chunks):
    time_count, cell_count = footprint.shape
    lat_count = lat_cov.shape[0]
    lon_count = lon_cov.shape[0]
    per, main_cols, full_rows, share, extra = layout_of(time_count, cell_count, chunks)
    along_lon = jnp.dot(
        footprint.reshape(time_count * lat_count, lon_count),
        lon_cov,
        preferred_element_type=jnp.float32,
    ).astype(jnp.bfloat16)
    along_lat = jnp.einsum(
        "tab,ac->tcb",
        along_lon.reshape(time_count, lat_count, lon_count),
        lat_cov,
        preferred_element_type=jnp.float32,
    ).astype(jnp.bfloat16)
    along_lat = along_lat.reshape(time_count, cell_count)
    main = along_lat[:, :main_cols].reshape(time_count, chunks * per, LANE)
    main = jnp.einsum("ts,tjl->jsl", time_cov[:, :full_rows], main, preferred_element_type=jnp.float32)
    main = main.astype(jnp.bfloat16).reshape(chunks, per * full_rows, LANE)
    low = jnp.dot(time_cov[:, full_rows:].T, along_lat[:, :main_cols], preferred_element_type=jnp.float32)
    right = jnp.dot(time_cov.T, along_lat[:, main_cols:], preferred_element_type=jnp.float32)
    rest = rest_chunks(low.astype(jnp.bfloat16), right.astype(jnp.bfloat16), chunks, share)
    return assemble(main, rest, extra, chunks, jnp.bfloat16)


def local(footprints, time_cov, lat_cov, lon_cov):
    space_count = lax.axis_size("space")
    rec_count = lax.axis_size("rec")
    rec_index = lax.axis_index("rec")
    plain = dense_chunks(footprints[0], space_count)
    plain, footprint = lax.optimization_barrier((plain, footprints[0]))
    plain_here = lax.all_to_all(plain, "space", split_axis=0, concat_axis=0, tiled=True)
    weighted = weighted_dense_chunks(footprint, time_cov, lat_cov, lon_cov, space_count)
    weighted_here = lax.all_to_all(weighted, "space", split_axis=0, concat_axis=0, tiled=True)
    contract = (((1, 2), (1, 2)), ((), ()))
    group = plain_here.shape[0]
    received = [plain_here]
    for shift in range(1, rec_count):
        perm = [(i, (i + shift) % rec_count) for i in range(rec_count)]
        received.append(lax.ppermute(plain_here, "rec", perm))
    blocks = [lax.dot_general(weighted_here, part, contract, preferred_element_type=jnp.float32) for part in received]
    ordered = []
    for g in range(rec_count):
        choice = blocks[0]
        for shift in range(1, rec_count):
            choice = jnp.where((rec_index + rec_count - shift) % rec_count == g, blocks[shift], choice)
        ordered.append(choice)
    partial_value = jnp.concatenate(ordered, axis=1)
    spread = lax.all_to_all(partial_value, "space", split_axis=0, concat_axis=0, tiled=True)
    return jnp.sum(spread, axis=0, keepdims=True)


def solution(mesh):
    in_specs = (P(("rec", "space"), None, None), P(), P(), P())
    out_specs = P(("rec", "space"), None)
    return jax.shard_map(local, mesh=mesh, in_specs=in_specs, out_specs=out_specs, check_vma=False)
```

```python
import functools
import jax
import jax.numpy as jnp
from jax import lax
from jax.sharding import PartitionSpec as P
from jax.experimental import pallas as pl
from jax.experimental.pallas import tpu as pltpu

ROW_TILE = 16
LANE = 128


def layout_of(time_count, cell_count, chunks):
    col_tiles = cell_count // LANE
    per = col_tiles // chunks
    main_cols = per * chunks * LANE
    full_rows = (time_count // ROW_TILE) * ROW_TILE
    rest_rows = (time_count - full_rows) * (main_cols // LANE)
    rest_rows += time_count * (-(-(cell_count - main_cols) // LANE))
    share = -(-rest_rows // chunks)
    rows = per * full_rows + share
    padded_rows = -(-rows // ROW_TILE) * ROW_TILE
    return per, main_cols, full_rows, share, padded_rows - rows


def rest_chunks(low, right, chunks, share):
    parts = []
    if low.shape[0]:
        height = low.shape[0]
        parts.append(low.reshape(height, -1, LANE).transpose(1, 0, 2).reshape(-1, LANE))
    if right.shape[1]:
        height, width = right.shape
        tiles = -(-width // LANE)
        right = jnp.pad(right, ((0, 0), (0, tiles * LANE - width)))
        parts.append(right.reshape(height, tiles, LANE).transpose(1, 0, 2).reshape(-1, LANE))
    rest = jnp.concatenate(parts, axis=0)
    rest = jnp.pad(rest, ((0, share * chunks - rest.shape[0]), (0, 0)))
    return rest.reshape(chunks, share, LANE)


def assemble(main, rest, extra, chunks, dtype):
    pieces = [main, rest]
    if extra:
        pieces.append(jnp.zeros((chunks, extra, LANE), dtype))
    return jnp.concatenate(pieces, axis=1)


def pack_kernel(full_rows, per, share, values_hbm, out_hbm, values, rest_out, rest_ref, in_sems, out_sems):
    time_count, cell_count = values.shape
    chunks, rows, _ = out_hbm.shape
    main_tiles = chunks * per
    main_cols = main_tiles * LANE
    groups = 4 if chunks % 4 == 0 else 1
    width = main_cols // groups
    loads = []
    for g in range(groups):
        load = pltpu.make_async_copy(
            values_hbm.at[:, g * width:(g + 1) * width], values.at[:, g * width:(g + 1) * width], in_sems.at[g]
        )
        load.start()
        loads.append(load)
    if cell_count > main_cols:
        tail = pltpu.make_async_copy(
            values_hbm.at[:, main_cols:cell_count], values.at[:, main_cols:cell_count], in_sems.at[groups]
        )
        tail.start()
        loads.append(tail)
    stores = []
    per_group = chunks // groups
    for g in range(groups):
        loads[g].wait()
        for k in range(g * per_group, (g + 1) * per_group):
            for q in range(per):
                j = k * per + q
                store = pltpu.make_async_copy(
                    values.at[0:full_rows, j * LANE:(j + 1) * LANE],
                    out_hbm.at[k, q * full_rows:(q + 1) * full_rows, :],
                    out_sems.at[j],
                )
                store.start()
                stores.append(store)
    if cell_count > main_cols:
        loads[groups].wait()
    rest_ref[...] = jnp.zeros(rest_ref.shape, rest_ref.dtype)
    low = time_count - full_rows
    at = 0
    if low:
        for j in range(main_tiles):
            rest_ref[at:at + low, :] = values[full_rows:time_count, j * LANE:(j + 1) * LANE].astype(jnp.float32)
            at += low
    for lo in range(main_cols, cell_count, LANE):
        span = min(LANE, cell_count - lo)
        rest_ref[at:at + time_count, 0:span] = values[:, lo:lo + span].astype(jnp.float32)
        at += time_count
    tail_rows = rows - per * full_rows
    for k in range(chunks):
        rest_out[k, 0:share, :] = rest_ref[k * share:(k + 1) * share, :].astype(rest_out.dtype)
        if tail_rows > share:
            rest_out[k, share:, :] = jnp.zeros((tail_rows - share, LANE), rest_out.dtype)
    last = pltpu.make_async_copy(rest_out, out_hbm.at[:, per * full_rows:rows, :], out_sems.at[main_tiles])
    last.start()
    for store in stores:
        store.wait()
    last.wait()


def dense_chunks(values, chunks):
    time_count, cell_count = values.shape
    per, main_cols, full_rows, share, extra = layout_of(time_count, cell_count, chunks)
    rows = per * full_rows + share + extra
    return pl.pallas_call(
        functools.partial(pack_kernel, full_rows, per, share),
        out_shape=jax.ShapeDtypeStruct((chunks, rows, LANE), values.dtype),
        in_specs=[pl.BlockSpec(memory_space=pl.ANY)],
        out_specs=pl.BlockSpec(memory_space=pl.ANY),
        scratch_shapes=[
            pltpu.VMEM((time_count, cell_count), values.dtype),
            pltpu.VMEM((chunks, rows - per * full_rows, LANE), values.dtype),
            pltpu.VMEM((share * chunks, LANE), jnp.float32),
            pltpu.SemaphoreType.DMA((5,)),
            pltpu.SemaphoreType.DMA((chunks * per + 1,)),
        ],
        cost_estimate=pl.CostEstimate(flops=0, transcendentals=0, bytes_accessed=4 * chunks * rows * LANE),
    )(values)


def weighted_dense_chunks(footprint, time_cov, lat_cov, lon_cov, chunks):
    time_count, cell_count = footprint.shape
    lat_count = lat_cov.shape[0]
    lon_count = lon_cov.shape[0]
    per, main_cols, full_rows, share, extra = layout_of(time_count, cell_count, chunks)
    along_lon = jnp.dot(
        footprint.reshape(time_count * lat_count, lon_count),
        lon_cov,
        preferred_element_type=jnp.float32,
    ).astype(jnp.bfloat16)
    along_lat = jnp.einsum(
        "tab,ac->tcb",
        along_lon.reshape(time_count, lat_count, lon_count),
        lat_cov,
        preferred_element_type=jnp.float32,
    ).astype(jnp.bfloat16)
    along_lat = along_lat.reshape(time_count, cell_count)
    main = along_lat[:, :main_cols].reshape(time_count, chunks * per, LANE)
    main = jnp.einsum("ts,tjl->jsl", time_cov[:, :full_rows], main, preferred_element_type=jnp.float32)
    main = main.astype(jnp.bfloat16).reshape(chunks, per * full_rows, LANE)
    low = jnp.dot(time_cov[:, full_rows:].T, along_lat[:, :main_cols], preferred_element_type=jnp.float32)
    right = jnp.dot(time_cov.T, along_lat[:, main_cols:], preferred_element_type=jnp.float32)
    rest = rest_chunks(low.astype(jnp.bfloat16), right.astype(jnp.bfloat16), chunks, share)
    return assemble(main, rest, extra, chunks, jnp.bfloat16)


def local(footprints, time_cov, lat_cov, lon_cov):
    space_count = lax.axis_size("space")
    rec_count = lax.axis_size("rec")
    rec_index = lax.axis_index("rec")
    plain = dense_chunks(footprints[0], space_count)
    plain, footprint = lax.optimization_barrier((plain, footprints[0]))
    plain_here = lax.all_to_all(plain, "space", split_axis=0, concat_axis=0, tiled=True)
    weighted = weighted_dense_chunks(footprint, time_cov, lat_cov, lon_cov, space_count)
    weighted_here = lax.all_to_all(weighted, "space", split_axis=0, concat_axis=0, tiled=True)
    contract = (((1, 2), (1, 2)), ((), ()))
    group = plain_here.shape[0]
    received = [plain_here]
    for shift in range(1, rec_count):
        perm = [(i, (i + shift) % rec_count) for i in range(rec_count)]
        received.append(lax.ppermute(plain_here, "rec", perm))
    ordered = []
    for g in range(rec_count):
        choice = received[0]
        for shift in range(1, rec_count):
            choice = jnp.where((rec_index + rec_count - shift) % rec_count == g, received[shift], choice)
        ordered.append(choice)
    everyone = jnp.concatenate(ordered, axis=0)
    partial_value = lax.dot_general(weighted_here, everyone, contract, preferred_element_type=jnp.float32)
    spread = lax.all_to_all(partial_value, "space", split_axis=0, concat_axis=0, tiled=True)
    return jnp.sum(spread, axis=0, keepdims=True)


def solution(mesh):
    in_specs = (P(("rec", "space"), None, None), P(), P(), P())
    out_specs = P(("rec", "space"), None)
    return jax.shard_map(local, mesh=mesh, in_specs=in_specs, out_specs=out_specs, check_vma=False)
```

```python
import functools
import jax
import jax.numpy as jnp
from jax import lax
from jax.sharding import PartitionSpec as P
from jax.experimental import pallas as pl
from jax.experimental.pallas import tpu as pltpu

ROW_TILE = 16
LANE = 128


def layout_of(time_count, cell_count, chunks):
    col_tiles = cell_count // LANE
    per = col_tiles // chunks
    main_cols = per * chunks * LANE
    full_rows = (time_count // ROW_TILE) * ROW_TILE
    rest_rows = (time_count - full_rows) * (main_cols // LANE)
    rest_rows += time_count * (-(-(cell_count - main_cols) // LANE))
    share = -(-rest_rows // chunks)
    rows = per * full_rows + share
    padded_rows = -(-rows // ROW_TILE) * ROW_TILE
    return per, main_cols, full_rows, share, padded_rows - rows


def rest_chunks(low, right, chunks, share):
    parts = []
    if low.shape[0]:
        height = low.shape[0]
        parts.append(low.reshape(height, -1, LANE).transpose(1, 0, 2).reshape(-1, LANE))
    if right.shape[1]:
        height, width = right.shape
        tiles = -(-width // LANE)
        right = jnp.pad(right, ((0, 0), (0, tiles * LANE - width)))
        parts.append(right.reshape(height, tiles, LANE).transpose(1, 0, 2).reshape(-1, LANE))
    rest = jnp.concatenate(parts, axis=0)
    rest = jnp.pad(rest, ((0, share * chunks - rest.shape[0]), (0, 0)))
    return rest.reshape(chunks, share, LANE)


def assemble(main, rest, extra, chunks, dtype):
    pieces = [main, rest]
    if extra:
        pieces.append(jnp.zeros((chunks, extra, LANE), dtype))
    return jnp.concatenate(pieces, axis=1)


def pack_kernel(full_rows, per, share, values_hbm, out_hbm, values, main_out, rest_out, rest_ref, in_sems, out_sems):
    time_count, cell_count = values.shape
    chunks, rows, _ = out_hbm.shape
    main_tiles = chunks * per
    main_cols = main_tiles * LANE
    groups = 4 if chunks % 4 == 0 else 1
    width = main_cols // groups
    loads = []
    for g in range(groups):
        load = pltpu.make_async_copy(
            values_hbm.at[:, g * width:(g + 1) * width], values.at[:, g * width:(g + 1) * width], in_sems.at[g]
        )
        load.start()
        loads.append(load)
    if cell_count > main_cols:
        tail = pltpu.make_async_copy(
            values_hbm.at[:, main_cols:cell_count], values.at[:, main_cols:cell_count], in_sems.at[groups]
        )
        tail.start()
        loads.append(tail)
    stores = []
    per_group = chunks // groups
    for g in range(groups):
        loads[g].wait()
        for k in range(g * per_group, (g + 1) * per_group):
            for q in range(per):
                j = k * per + q
                main_out[k, q * full_rows:(q + 1) * full_rows, :] = values[0:full_rows, j * LANE:(j + 1) * LANE]
        store = pltpu.make_async_copy(
            main_out.at[g * per_group:(g + 1) * per_group],
            out_hbm.at[g * per_group:(g + 1) * per_group, 0:per * full_rows, :],
            out_sems.at[g],
        )
        store.start()
        stores.append(store)
    if cell_count > main_cols:
        loads[groups].wait()
    rest_ref[...] = jnp.zeros(rest_ref.shape, rest_ref.dtype)
    low = time_count - full_rows
    at = 0
    if low:
        for j in range(main_tiles):
            rest_ref[at:at + low, :] = values[full_rows:time_count, j * LANE:(j + 1) * LANE].astype(jnp.float32)
            at += low
    for lo in range(main_cols, cell_count, LANE):
        span = min(LANE, cell_count - lo)
        rest_ref[at:at + time_count, 0:span] = values[:, lo:lo + span].astype(jnp.float32)
        at += time_count
    tail_rows = rows - per * full_rows
    for k in range(chunks):
        rest_out[k, 0:share, :] = rest_ref[k * share:(k + 1) * share, :].astype(rest_out.dtype)
        if tail_rows > share:
            rest_out[k, share:, :] = jnp.zeros((tail_rows - share, LANE), rest_out.dtype)
    last = pltpu.make_async_copy(rest_out, out_hbm.at[:, per * full_rows:rows, :], out_sems.at[groups])
    last.start()
    for store in stores:
        store.wait()
    last.wait()


def dense_chunks(values, chunks):
    time_count, cell_count = values.shape
    per, main_cols, full_rows, share, extra = layout_of(time_count, cell_count, chunks)
    rows = per * full_rows + share + extra
    return pl.pallas_call(
        functools.partial(pack_kernel, full_rows, per, share),
        out_shape=jax.ShapeDtypeStruct((chunks, rows, LANE), values.dtype),
        in_specs=[pl.BlockSpec(memory_space=pl.ANY)],
        out_specs=pl.BlockSpec(memory_space=pl.ANY),
        scratch_shapes=[
            pltpu.VMEM((time_count, cell_count), values.dtype),
            pltpu.VMEM((chunks, per * full_rows, LANE), values.dtype),
            pltpu.VMEM((chunks, rows - per * full_rows, LANE), values.dtype),
            pltpu.VMEM((share * chunks, LANE), jnp.float32),
            pltpu.SemaphoreType.DMA((5,)),
            pltpu.SemaphoreType.DMA((5,)),
        ],
        cost_estimate=pl.CostEstimate(flops=0, transcendentals=0, bytes_accessed=4 * chunks * rows * LANE),
    )(values)


def weighted_dense_chunks(footprint, time_cov, lat_cov, lon_cov, chunks):
    time_count, cell_count = footprint.shape
    lat_count = lat_cov.shape[0]
    lon_count = lon_cov.shape[0]
    per, main_cols, full_rows, share, extra = layout_of(time_count, cell_count, chunks)
    along_lon = jnp.dot(
        footprint.reshape(time_count * lat_count, lon_count),
        lon_cov,
        preferred_element_type=jnp.float32,
    ).astype(jnp.bfloat16)
    along_lat = jnp.einsum(
        "tab,ac->tcb",
        along_lon.reshape(time_count, lat_count, lon_count),
        lat_cov,
        preferred_element_type=jnp.float32,
    ).astype(jnp.bfloat16)
    along_lat = along_lat.reshape(time_count, cell_count)
    main = along_lat[:, :main_cols].reshape(time_count, chunks * per, LANE)
    main = jnp.einsum("ts,tjl->jsl", time_cov[:, :full_rows], main, preferred_element_type=jnp.float32)
    main = main.astype(jnp.bfloat16).reshape(chunks, per * full_rows, LANE)
    low = jnp.dot(time_cov[:, full_rows:].T, along_lat[:, :main_cols], preferred_element_type=jnp.float32)
    right = jnp.dot(time_cov.T, along_lat[:, main_cols:], preferred_element_type=jnp.float32)
    rest = rest_chunks(low.astype(jnp.bfloat16), right.astype(jnp.bfloat16), chunks, share)
    return assemble(main, rest, extra, chunks, jnp.bfloat16)


def local(footprints, time_cov, lat_cov, lon_cov):
    space_count = lax.axis_size("space")
    rec_count = lax.axis_size("rec")
    rec_index = lax.axis_index("rec")
    plain = dense_chunks(footprints[0], space_count)
    plain, footprint = lax.optimization_barrier((plain, footprints[0]))
    plain_here = lax.all_to_all(plain, "space", split_axis=0, concat_axis=0, tiled=True)
    weighted = weighted_dense_chunks(footprint, time_cov, lat_cov, lon_cov, space_count)
    weighted_here = lax.all_to_all(weighted, "space", split_axis=0, concat_axis=0, tiled=True)
    contract = (((1, 2), (1, 2)), ((), ()))
    group = plain_here.shape[0]
    received = [plain_here]
    for shift in range(1, rec_count):
        perm = [(i, (i + shift) % rec_count) for i in range(rec_count)]
        received.append(lax.ppermute(plain_here, "rec", perm))
    ordered = []
    for g in range(rec_count):
        choice = received[0]
        for shift in range(1, rec_count):
            choice = jnp.where((rec_index + rec_count - shift) % rec_count == g, received[shift], choice)
        ordered.append(choice)
    everyone = jnp.concatenate(ordered, axis=0)
    partial_value = lax.dot_general(weighted_here, everyone, contract, preferred_element_type=jnp.float32)
    spread = lax.all_to_all(partial_value, "space", split_axis=0, concat_axis=0, tiled=True)
    ones = jnp.ones((1, spread.shape[0]), jnp.float32)
    return jnp.dot(ones, spread, precision=lax.Precision.HIGHEST, preferred_element_type=jnp.float32)


def solution(mesh):
    in_specs = (P(("rec", "space"), None, None), P(), P(), P())
    out_specs = P(("rec", "space"), None)
    return jax.shard_map(local, mesh=mesh, in_specs=in_specs, out_specs=out_specs, check_vma=False)
```

```python
import functools
import jax
import jax.numpy as jnp
from jax import lax
from jax.sharding import PartitionSpec as P
from jax.experimental import pallas as pl
from jax.experimental.pallas import tpu as pltpu

ROW_TILE = 16
LANE = 128


def layout_of(time_count, cell_count, chunks):
    col_tiles = cell_count // LANE
    per = col_tiles // chunks
    main_cols = per * chunks * LANE
    full_rows = (time_count // ROW_TILE) * ROW_TILE
    rest_rows = (time_count - full_rows) * (main_cols // LANE)
    rest_rows += time_count * (-(-(cell_count - main_cols) // LANE))
    share = -(-rest_rows // chunks)
    rows = per * full_rows + share
    padded_rows = -(-rows // ROW_TILE) * ROW_TILE
    return per, main_cols, full_rows, share, padded_rows - rows


def rest_chunks(low, right, chunks, share):
    parts = []
    if low.shape[0]:
        height = low.shape[0]
        parts.append(low.reshape(height, -1, LANE).transpose(1, 0, 2).reshape(-1, LANE))
    if right.shape[1]:
        height, width = right.shape
        tiles = -(-width // LANE)
        right = jnp.pad(right, ((0, 0), (0, tiles * LANE - width)))
        parts.append(right.reshape(height, tiles, LANE).transpose(1, 0, 2).reshape(-1, LANE))
    rest = jnp.concatenate(parts, axis=0)
    rest = jnp.pad(rest, ((0, share * chunks - rest.shape[0]), (0, 0)))
    return rest.reshape(chunks, share, LANE)


def assemble(main, rest, extra, chunks, dtype):
    pieces = [main, rest]
    if extra:
        pieces.append(jnp.zeros((chunks, extra, LANE), dtype))
    return jnp.concatenate(pieces, axis=1)


def pack_kernel(full_rows, per, share, values_hbm, out_hbm, values, main_out, rest_out, rest_ref, in_sems, out_sems):
    time_count, cell_count = values.shape
    chunks, rows, _ = out_hbm.shape
    main_tiles = chunks * per
    main_cols = main_tiles * LANE
    groups = 2 if chunks % 2 == 0 else 1
    width = main_cols // groups
    loads = []
    for g in range(groups):
        load = pltpu.make_async_copy(
            values_hbm.at[:, g * width:(g + 1) * width], values.at[:, g * width:(g + 1) * width], in_sems.at[g]
        )
        load.start()
        loads.append(load)
    if cell_count > main_cols:
        tail = pltpu.make_async_copy(
            values_hbm.at[:, main_cols:cell_count], values.at[:, main_cols:cell_count], in_sems.at[groups]
        )
        tail.start()
        loads.append(tail)
    stores = []
    per_group = chunks // groups
    for g in range(groups):
        loads[g].wait()
        for k in range(g * per_group, (g + 1) * per_group):
            for q in range(per):
                j = k * per + q
                main_out[k, q * full_rows:(q + 1) * full_rows, :] = values[0:full_rows, j * LANE:(j + 1) * LANE]
        store = pltpu.make_async_copy(
            main_out.at[g * per_group:(g + 1) * per_group],
            out_hbm.at[g * per_group:(g + 1) * per_group, 0:per * full_rows, :],
            out_sems.at[g],
        )
        store.start()
        stores.append(store)
    if cell_count > main_cols:
        loads[groups].wait()
    rest_ref[...] = jnp.zeros(rest_ref.shape, rest_ref.dtype)
    low = time_count - full_rows
    at = 0
    if low:
        for j in range(main_tiles):
            rest_ref[at:at + low, :] = values[full_rows:time_count, j * LANE:(j + 1) * LANE].astype(jnp.float32)
            at += low
    for lo in range(main_cols, cell_count, LANE):
        span = min(LANE, cell_count - lo)
        rest_ref[at:at + time_count, 0:span] = values[:, lo:lo + span].astype(jnp.float32)
        at += time_count
    tail_rows = rows - per * full_rows
    for k in range(chunks):
        rest_out[k, 0:share, :] = rest_ref[k * share:(k + 1) * share, :].astype(rest_out.dtype)
        if tail_rows > share:
            rest_out[k, share:, :] = jnp.zeros((tail_rows - share, LANE), rest_out.dtype)
    last = pltpu.make_async_copy(rest_out, out_hbm.at[:, per * full_rows:rows, :], out_sems.at[groups])
    last.start()
    for store in stores:
        store.wait()
    last.wait()


def dense_chunks(values, chunks):
    time_count, cell_count = values.shape
    per, main_cols, full_rows, share, extra = layout_of(time_count, cell_count, chunks)
    rows = per * full_rows + share + extra
    return pl.pallas_call(
        functools.partial(pack_kernel, full_rows, per, share),
        out_shape=jax.ShapeDtypeStruct((chunks, rows, LANE), values.dtype),
        in_specs=[pl.BlockSpec(memory_space=pl.ANY)],
        out_specs=pl.BlockSpec(memory_space=pl.ANY),
        scratch_shapes=[
            pltpu.VMEM((time_count, cell_count), values.dtype),
            pltpu.VMEM((chunks, per * full_rows, LANE), values.dtype),
            pltpu.VMEM((chunks, rows - per * full_rows, LANE), values.dtype),
            pltpu.VMEM((share * chunks, LANE), jnp.float32),
            pltpu.SemaphoreType.DMA((5,)),
            pltpu.SemaphoreType.DMA((5,)),
        ],
        cost_estimate=pl.CostEstimate(flops=0, transcendentals=0, bytes_accessed=4 * chunks * rows * LANE),
    )(values)


def weighted_dense_chunks(footprint, time_cov, lat_cov, lon_cov, chunks):
    time_count, cell_count = footprint.shape
    lat_count = lat_cov.shape[0]
    lon_count = lon_cov.shape[0]
    per, main_cols, full_rows, share, extra = layout_of(time_count, cell_count, chunks)
    along_lon = jnp.dot(
        footprint.reshape(time_count * lat_count, lon_count),
        lon_cov,
        preferred_element_type=jnp.float32,
    ).astype(jnp.bfloat16)
    along_lat = jnp.einsum(
        "tab,ac->tcb",
        along_lon.reshape(time_count, lat_count, lon_count),
        lat_cov,
        preferred_element_type=jnp.float32,
    ).astype(jnp.bfloat16)
    along_lat = along_lat.reshape(time_count, cell_count)
    main = along_lat[:, :main_cols].reshape(time_count, chunks * per, LANE)
    main = jnp.einsum("ts,tjl->jsl", time_cov[:, :full_rows], main, preferred_element_type=jnp.float32)
    main = main.astype(jnp.bfloat16).reshape(chunks, per * full_rows, LANE)
    low = jnp.dot(time_cov[:, full_rows:].T, along_lat[:, :main_cols], preferred_element_type=jnp.float32)
    right = jnp.dot(time_cov.T, along_lat[:, main_cols:], preferred_element_type=jnp.float32)
    rest = rest_chunks(low.astype(jnp.bfloat16), right.astype(jnp.bfloat16), chunks, share)
    return assemble(main, rest, extra, chunks, jnp.bfloat16)


def local(footprints, time_cov, lat_cov, lon_cov):
    space_count = lax.axis_size("space")
    rec_count = lax.axis_size("rec")
    rec_index = lax.axis_index("rec")
    plain = dense_chunks(footprints[0], space_count)
    plain, footprint = lax.optimization_barrier((plain, footprints[0]))
    plain_here = lax.all_to_all(plain, "space", split_axis=0, concat_axis=0, tiled=True)
    weighted = weighted_dense_chunks(footprint, time_cov, lat_cov, lon_cov, space_count)
    weighted_here = lax.all_to_all(weighted, "space", split_axis=0, concat_axis=0, tiled=True)
    contract = (((1, 2), (1, 2)), ((), ()))
    group = plain_here.shape[0]
    received = [plain_here]
    for shift in range(1, rec_count):
        perm = [(i, (i + shift) % rec_count) for i in range(rec_count)]
        received.append(lax.ppermute(plain_here, "rec", perm))
    ordered = []
    for g in range(rec_count):
        choice = received[0]
        for shift in range(1, rec_count):
            choice = jnp.where((rec_index + rec_count - shift) % rec_count == g, received[shift], choice)
        ordered.append(choice)
    everyone = jnp.concatenate(ordered, axis=0)
    partial_value = lax.dot_general(weighted_here, everyone, contract, preferred_element_type=jnp.float32)
    spread = lax.all_to_all(partial_value, "space", split_axis=0, concat_axis=0, tiled=True)
    return jnp.sum(spread, axis=0, keepdims=True)


def solution(mesh):
    in_specs = (P(("rec", "space"), None, None), P(), P(), P())
    out_specs = P(("rec", "space"), None)
    return jax.shard_map(local, mesh=mesh, in_specs=in_specs, out_specs=out_specs, check_vma=False)
```
